256 devices in a mesh: rep: 16 (over z, core), exp: 16 (over y, x).
Axes of the slice: x: 4, y: 4, z: 8, core: 2. Of those that a mesh axis runs over, the one named last changes fastest.
Arguments:
- tokens: bfloat16 [2048, 2048], P('exp'), may hold values from -6 to 6
- expert_ids: int32 [2048, 2], P('exp'), may hold values from 0 to 15, all different within a row; in each aligned block of 128 rows (0 to 127, 128 to 255, ...) at most 32 rows name the same one
- gate_values: float32 [2048, 2], P('exp'), may hold values from 0.2 to 1
- grad_out: bfloat16 [2048, 2048], P('exp'), may hold values from -6 to 6
- w_up: bfloat16 [16, 2048, 8192], P('exp', None, 'rep'), may hold values from -0.125 to 0.125
- w_down: bfloat16 [16, 8192, 2048], P('exp', 'rep'), may hold values from -0.0625 to 0.0625
Outputs:
- mixed: bfloat16 [2048, 2048], P('exp', 'rep')
- grad_tokens: bfloat16 [2048, 2048], P('exp', 'rep')
- grad_w_up: bfloat16 [16, 2048, 8192], P('exp', None, 'rep')
- grad_w_down: bfloat16 [16, 8192, 2048], P('exp', 'rep')
The draws below stay inside these ranges and needn't reach their ends.
Inputs may be any that keep to these rules, and one draw needn't show every extreme that they name: `expert_ids`: each row names 2 different experts. Within the rows of one index of exp (aligned blocks of 128 rows) no expert is named by more than 32 rows, a bound that some block reaches.
All inputs are finite; a program needn't handle non-finite values.
Results may differ from the reference program's by a relative error of at most 0.022.
Values may be sent and summed in bfloat16 or wider, within the bound.
No kernel may reach another device: no remote copies, remote signals or barrier semaphores. Data moves between devices by JAX's collectives and lax.ppermute only.
A program may use at most 128 MiB of HBM per device.

```python
import math
import jax
import jax.numpy as jnp
import numpy as np
from jax import lax

D = 2048
FF = 8192
TOP = 2
TOK_DEV = 128
EXPERTS = 16
EXPERT_SLOTS = 32
TOKENS = 2048
N_REP = 16
N_EXP = 16


def shard_levels(stream_key, extent, cuts, low, top_value):
    def one(axis_at, blocks):
        heights = jax.random.uniform(jax.random.fold_in(jax.random.fold_in(stream_key, 6), axis_at), (blocks,), jnp.float32, low / len(cuts), top_value / len(cuts))
        return jnp.repeat(jnp.exp(heights), extent[axis_at] // blocks).reshape((-1,) + (1,) * (len(extent) - axis_at - 1))

    loudness = one(*cuts[0])
    for cut in cuts[1:]:
        loudness = loudness * one(*cut)
    return loudness


def deal_out(rng, own, number, rows, amount, top, limit, lean):
    ranking = jax.random.permutation(rng, amount)
    packed, usual = shares(amount, rows * top, limit, lean, True), shares(amount, rows * top, limit, lean, False)
    places = jnp.arange(amount)

    def named(lengths, turn):
        used = int((lengths > 0).sum())
        fixed = max(1, used // 4)
        passed = fixed + (places - fixed + turn * (used - fixed)) % max(1, amount - fixed)
        return jnp.zeros((amount,), jnp.int32).at[ranking[jnp.where(places < fixed, places, passed)]].set(jnp.asarray(lengths, jnp.int32))

    lengths = jnp.where(number % 4 == 0, named(packed, number // 4), named(usual, number - number // 4 - 1))
    mixed = jax.random.permutation(jax.random.fold_in(own, 3), amount)
    giver, sink = mixed[0:amount // 2 * 2:2], mixed[1:amount // 2 * 2:2]
    margin = jnp.minimum(lengths[giver] - 1, limit - lengths[sink]) // 2
    margin = jnp.where((giver == ranking[0]) | (sink == ranking[0]) | (lengths[sink] == 0), 0, jnp.maximum(margin, 0))
    passed = jax.random.randint(jax.random.fold_in(own, 4), (amount // 2,), 0, 1 << 20) % (margin + 1)
    lengths = lengths.at[giver].add(-passed).at[sink].add(passed)
    items = jnp.searchsorted(jnp.cumsum(lengths), jnp.arange(rows * top), side="right").astype(jnp.int32)
    table = items.reshape(top, rows).T
    table = table[jax.random.permutation(jax.random.fold_in(own, 1), rows)]
    turn = jax.random.randint(jax.random.fold_in(own, 2), (rows, 1), 0, top)
    return jnp.take_along_axis(table, (jnp.arange(top)[None, :] + turn) % top, axis=1)


def shares(number_of, total, limit, skew, full):
    loads = [(1 << 20) // math.isqrt(grade ** skew) + 1 for grade in range(1, number_of + 1)]
    largest = limit if full else min(limit, max(-(-total // number_of), total * loads[0] // sum(loads)))
    least = 1 if total - largest >= number_of - 1 else 0
    given, surplus = [largest] + [least] * (number_of - 1), total - largest - least * (number_of - 1)
    while surplus > 0:
        candidates = [i for i in range(1, number_of) if given[i] < largest] or [i for i in range(1, number_of) if given[i] < limit]
        whole, left = sum([loads[i] for i in candidates]), surplus
        for i in candidates:
            more = min(limit - given[i], max(1, left * loads[i] // whole), surplus)
            given[i] = given[i] + more
            surplus = surplus - more
    return np.array(given)


def bell_draw(own_key, shape, width, reach, split=(), held_as=jnp.bfloat16):
    drawn = width * jax.random.normal(own_key, shape, jnp.float32)
    if split:
        drawn = drawn * shard_levels(own_key, shape, split, -0.22, 0.18)
    return jnp.clip(drawn, -reach, reach).astype(held_as)


def setup_inputs(seed: int = 0) -> dict:
    seeds = jax.random.split(jax.random.key(seed), 7)
    tokens = bell_draw(seeds[0], (TOKENS, D), 1.0, 6.0, ((0, 16),))
    expert_ids_keys = jax.random.split(jax.random.fold_in(seeds[1], 1), TOKENS // TOK_DEV)
    expert_ids_turns = jax.random.permutation(jax.random.fold_in(seeds[1], 3), TOKENS // TOK_DEV)
    expert_ids = jax.vmap(lambda own, number: deal_out(jax.random.fold_in(seeds[1], 2), own, number, TOK_DEV, EXPERTS, TOP, EXPERT_SLOTS, 1))(expert_ids_keys, expert_ids_turns).reshape((TOKENS, TOP))
    gate_values = jnp.clip(0.2 + 0.8 * jax.random.uniform(seeds[2], (TOKENS, TOP), jnp.float32) ** shard_levels(seeds[2], (TOKENS, TOP), ((0, 16),), -0.2, 0.2), 0.2, 1.0)
    grad_out = bell_draw(seeds[3], (TOKENS, D), 1.0, 6.0, ((0, 16),))
    w_up = bell_draw(seeds[4], (EXPERTS, D, FF), D ** -0.5, 0.125, ((0, 16), (2, 16)))
    w_down = bell_draw(seeds[5], (EXPERTS, FF, D), FF ** -0.5, 0.0625, ((0, 16), (1, 16)))
    return {"tokens": tokens, "expert_ids": expert_ids, "gate_values": gate_values, "grad_out": grad_out, "w_up": w_up, "w_down": w_down}


def silu_parts(preact):
    sigmoid_val = jax.nn.sigmoid(preact)
    return preact * sigmoid_val, sigmoid_val * (1.0 + preact * (1.0 - sigmoid_val))


def reference(tokens, expert_ids, gate_values, grad_out, w_up, w_down):
    device_total = N_EXP
    pair_count = TOK_DEV * TOP
    group_span_width = FF // N_REP
    expert_grid = expert_ids.reshape(device_total, pair_count)
    onehot = (expert_grid[:, :, None] == jnp.arange(EXPERTS, dtype=jnp.int32)[None, None, :]).astype(jnp.int32)
    before = jnp.cumsum(onehot, axis=1) - onehot
    position = jnp.sum(before * onehot, axis=2)
    device_ids = jnp.arange(device_total, dtype=jnp.int32)[:, None]
    slotting_labels = (device_ids * EXPERT_SLOTS + position).reshape(-1).astype(jnp.int32)
    flattened_experts = expert_grid.reshape(-1)
    pairing_total = device_total * pair_count
    slotting_total = device_total * EXPERT_SLOTS
    grad_rows = (gate_values[:, :, None] * grad_out[:, None, :].astype(jnp.float32)).astype(jnp.bfloat16)
    grad_rows = grad_rows.reshape(pairing_total, D)
    pairing_labels = jnp.arange(pairing_total, dtype=jnp.int32)

    def one_expert(expert_choice):
        destination = jnp.where(flattened_experts == expert_choice, slotting_labels, slotting_total).astype(jnp.int32)
        slotting_lookup = jnp.full((slotting_total,), pairing_total, dtype=jnp.int32).at[destination].set(pairing_labels, mode="drop")
        live_rows = slotting_lookup < pairing_total
        safe_rows = jnp.minimum(slotting_lookup, pairing_total - 1)
        zero_value = jnp.zeros((), jnp.bfloat16)
        rows_in = jnp.where(live_rows[:, None], tokens[safe_rows // TOP], zero_value)
        rows_grad = jnp.where(live_rows[:, None], grad_rows[safe_rows], zero_value)
        up_weight = w_up[expert_choice]
        down_weight = w_down[expert_choice]
        preact = jnp.dot(rows_in, up_weight, preferred_element_type=jnp.float32)
        value, slope = silu_parts(preact)
        hidden_units = value.astype(jnp.bfloat16)
        output_pieces = jnp.einsum("hkj,kjt->kht", hidden_units.reshape(slotting_total, N_REP, group_span_width).astype(jnp.float32),
                               down_weight.reshape(N_REP, group_span_width, D).astype(jnp.float32))
        output_pieces = lax.optimization_barrier(output_pieces.astype(jnp.bfloat16))
        out_row = jnp.sum(output_pieces.astype(jnp.float32), axis=0).astype(jnp.bfloat16)
        grad_hidden = jnp.dot(rows_grad, down_weight.T, preferred_element_type=jnp.float32)
        gradient_before_activation = (grad_hidden * slope).astype(jnp.bfloat16)
        grad_down_e = jnp.dot(hidden_units.T, rows_grad, preferred_element_type=jnp.float32).astype(jnp.bfloat16)
        grad_up_e = jnp.dot(rows_in.T, gradient_before_activation, preferred_element_type=jnp.float32).astype(jnp.bfloat16)
        input_grad_pieces = jnp.einsum("pbx,cbx->bpc", gradient_before_activation.reshape(slotting_total, N_REP, group_span_width).astype(jnp.float32),
                              up_weight.reshape(D, N_REP, group_span_width).astype(jnp.float32))
        input_grad_pieces = lax.optimization_barrier(input_grad_pieces.astype(jnp.bfloat16))
        dx_row = jnp.sum(input_grad_pieces.astype(jnp.float32), axis=0).astype(jnp.bfloat16)
        return out_row, dx_row, grad_up_e, grad_down_e

    out_rows, dx_rows, grad_w_up, grad_w_down = lax.map(one_expert, jnp.arange(EXPERTS, dtype=jnp.int32))
    pairing_index = (flattened_experts * slotting_total + slotting_labels).astype(jnp.int32)
    out_pairs = out_rows.reshape(-1, D)[pairing_index].astype(jnp.float32).reshape(TOKENS, TOP, D)
    mixed = jnp.sum(gate_values[:, :, None] * out_pairs, axis=1).astype(jnp.bfloat16)
    dx_pairs = dx_rows.reshape(-1, D)[pairing_index].astype(jnp.float32).reshape(TOKENS, TOP, D)
    grad_tokens = jnp.sum(dx_pairs, axis=1).astype(jnp.bfloat16)
    return mixed, grad_tokens, grad_w_up, grad_w_down
```

```python
import jax
import jax.numpy as jnp
from jax import lax
from jax.sharding import PartitionSpec as P


def plan_slots(routed, experts, capacity):
    flat_ids = routed.reshape(-1)
    onehot = (flat_ids[:, None] == jnp.arange(experts, dtype=jnp.int32)[None, :]).astype(jnp.int32)
    before = jnp.cumsum(onehot, axis=0) - onehot
    position = jnp.sum(before * onehot, axis=1)
    counts = jnp.sum(onehot, axis=0)
    slotting_labels = flat_ids * capacity + position
    placed = (
        slotting_labels[None, :] == jnp.arange(experts * capacity, dtype=jnp.int32)[:, None]
    ).astype(jnp.bfloat16)
    return (placed, counts)


def expert_math(rows_in, rows_grad, live_mask, up_weight, down_weight):
    preact = jnp.dot(rows_in, up_weight, preferred_element_type=jnp.float32)
    sigmoid_val = jax.nn.sigmoid(preact)
    keep = live_mask[:, None]
    hidden_units = jnp.where(keep, preact * sigmoid_val, 0.0).astype(jnp.bfloat16)
    out_part = jnp.dot(hidden_units, down_weight, preferred_element_type=jnp.float32)
    grad_hidden = lax.dot_general(
        rows_grad, down_weight, (((1,), (1,)), ((), ())), preferred_element_type=jnp.float32
    )
    slope = sigmoid_val * (1.0 + preact * (1.0 - sigmoid_val))
    gradient_before_activation = jnp.where(keep, grad_hidden * slope, 0.0).astype(jnp.bfloat16)
    grad_down_e = lax.dot_general(
        hidden_units, rows_grad, (((0,), (0,)), ((), ())), preferred_element_type=jnp.float32
    )
    grad_up_e = lax.dot_general(
        rows_in,
        gradient_before_activation,
        (((0,), (0,)), ((), ())),
        preferred_element_type=jnp.float32,
    )
    dx_part = lax.dot_general(
        gradient_before_activation,
        up_weight,
        (((1,), (1,)), ((), ())),
        preferred_element_type=jnp.float32,
    )
    return (out_part, dx_part, grad_up_e, grad_down_e)


def local(tokens, expert_ids, gate_values, grad_out, w_up, w_down):
    n_rep = lax.axis_size("rep")
    n_exp = lax.axis_size("exp")
    tok_count, width = tokens.shape
    top_k = expert_ids.shape[1]
    pair_count = tok_count * top_k
    capacity = max(2, min(tok_count, 2 * tok_count * top_k // n_exp))
    cols = width // n_rep
    up_weight = w_up[0]
    down_weight = w_down[0]
    grad_rows = (gate_values[:, :, None] * grad_out[:, None, :].astype(jnp.float32)).astype(
        jnp.bfloat16
    )
    grad_rows = grad_rows.reshape(pair_count, width)
    placed, counts = plan_slots(expert_ids, n_exp, capacity)
    summed = placed.reshape(n_exp * capacity, tok_count, top_k).sum(axis=2)
    sent_in = jnp.dot(summed, tokens, preferred_element_type=jnp.float32).astype(jnp.bfloat16)
    sent_grad = jnp.dot(placed, grad_rows, preferred_element_type=jnp.float32).astype(jnp.bfloat16)
    count_parts = jnp.stack([counts // 16, counts % 16], axis=1).astype(jnp.bfloat16)
    got_in, got_grad, got_counts = (
        lax.all_to_all(
            sent_in.reshape(n_exp, capacity, width), "exp", split_axis=0, concat_axis=0, tiled=True
        ),
        lax.all_to_all(
            sent_grad.reshape(n_exp, capacity, width),
            "exp",
            split_axis=0,
            concat_axis=0,
            tiled=True,
        ),
        lax.all_to_all(count_parts, "exp", split_axis=0, concat_axis=0, tiled=True),
    )
    count_values = got_counts[:, 0].astype(jnp.float32) * 16.0 + got_counts[:, 1].astype(
        jnp.float32
    )
    slot_mask = jnp.arange(capacity, dtype=jnp.float32)[None, :] < count_values[:, None]
    rows_in = got_in.reshape(-1, width)
    rows_grad = got_grad.reshape(-1, width)
    live_mask = slot_mask.reshape(-1)
    out_part, dx_part, grad_up_e, grad_down_e = expert_math(
        rows_in, rows_grad, live_mask, up_weight, down_weight
    )
    summed_out = lax.psum_scatter(
        out_part.astype(jnp.bfloat16), "rep", scatter_dimension=1, tiled=True
    )
    summed_dx = lax.psum_scatter(
        dx_part.astype(jnp.bfloat16), "rep", scatter_dimension=1, tiled=True
    )
    both = jnp.concatenate([summed_out, summed_dx], axis=1)
    back_both = lax.all_to_all(
        both.reshape(n_exp, capacity, 2 * cols), "exp", split_axis=0, concat_axis=0, tiled=True
    ).reshape(n_exp * capacity, 2 * cols)
    back_out = back_both[:, :cols]
    back_dx = back_both[:, cols:]
    pair_out = jnp.einsum(
        "st,sd->td",
        placed,
        back_out.reshape(n_exp * capacity, cols),
        preferred_element_type=jnp.float32,
    )
    pair_dx = jnp.einsum(
        "st,sd->td",
        placed,
        back_dx.reshape(n_exp * capacity, cols),
        preferred_element_type=jnp.float32,
    )
    mixed = jnp.sum(gate_values[:, :, None] * pair_out.reshape(tok_count, top_k, cols), axis=1)
    grad_tokens = jnp.sum(pair_dx.reshape(tok_count, top_k, cols), axis=1)
    return (
        mixed.astype(jnp.bfloat16),
        grad_tokens.astype(jnp.bfloat16),
        grad_up_e.astype(jnp.bfloat16)[None],
        grad_down_e.astype(jnp.bfloat16)[None],
    )


def solution(mesh):
    return jax.shard_map(
        local,
        mesh=mesh,
        in_specs=(
            P("exp", None),
            P("exp", None),
            P("exp", None),
            P("exp", None),
            P("exp", None, "rep"),
            P("exp", "rep", None),
        ),
        out_specs=(P("exp", "rep"), P("exp", "rep"), P("exp", None, "rep"), P("exp", "rep", None)),
        check_vma=False,
    )
```

```python
import jax
import jax.numpy as jnp
from jax import lax
from jax.sharding import Mesh, PartitionSpec as P


def plan_slots(routed, experts, capacity):
    flat_ids = routed.reshape(-1)
    onehot = (flat_ids[:, None] == jnp.arange(experts, dtype=jnp.int32)[None, :]).astype(jnp.int32)
    before = jnp.cumsum(onehot, axis=0) - onehot
    position = jnp.sum(before * onehot, axis=1)
    counts = jnp.sum(onehot, axis=0)
    slotting_labels = flat_ids * capacity + position
    placed = (
        slotting_labels[None, :] == jnp.arange(experts * capacity, dtype=jnp.int32)[:, None]
    ).astype(jnp.bfloat16)
    return (placed, counts)


def expert_math(rows_in, rows_grad, live_mask, up_weight, down_weight, up_perm, down_perm):
    preact = jnp.dot(rows_in, up_weight, preferred_element_type=jnp.float32)
    sigmoid_val = jax.nn.sigmoid(preact)
    keep = live_mask[:, None]
    hidden_units = jnp.where(keep, preact * sigmoid_val, 0.0).astype(jnp.bfloat16)
    out_part = jnp.dot(hidden_units, down_perm, preferred_element_type=jnp.float32)
    grad_hidden = lax.dot_general(
        rows_grad, down_weight, (((1,), (1,)), ((), ())), preferred_element_type=jnp.float32
    )
    slope = sigmoid_val * (1.0 + preact * (1.0 - sigmoid_val))
    gradient_before_activation = jnp.where(keep, grad_hidden * slope, 0.0).astype(jnp.bfloat16)
    dx_part = lax.dot_general(
        gradient_before_activation,
        up_perm,
        (((1,), (1,)), ((), ())),
        preferred_element_type=jnp.float32,
    )
    grad_down_e = lax.dot_general(
        hidden_units, rows_grad, (((0,), (0,)), ((), ())), preferred_element_type=jnp.float32
    )
    grad_up_e = lax.dot_general(
        rows_in,
        gradient_before_activation,
        (((0,), (0,)), ((), ())),
        preferred_element_type=jnp.float32,
    )
    return (out_part, dx_part, grad_up_e, grad_down_e)


def pick(stacked, index, axis):
    return lax.dynamic_index_in_dim(stacked, index, axis=axis, keepdims=False)


def reduce_over_rep(part, n_z, n_core, cols):
    slots = part.shape[0]
    core = lax.axis_index("core")
    zi = lax.axis_index("z")
    halves = part.reshape(slots, n_core, n_z * cols)
    mine = pick(halves, core, 1)
    other = pick(halves, (core + 1) % n_core, 1)
    got = lax.ppermute(other, "core", [(j, (j + 1) % n_core) for j in range(n_core)])
    pair_sum = (mine.astype(jnp.float32) + got.astype(jnp.float32)).astype(jnp.bfloat16)
    blocks = pair_sum.reshape(slots, n_z, cols)
    acc = pick(blocks, zi, 1).astype(jnp.float32)
    for k in range(1, n_z):
        piece = pick(blocks, (zi + k) % n_z, 1)
        moved = lax.ppermute(piece, "z", [(j, (j + k) % n_z) for j in range(n_z)])
        acc = acc + moved.astype(jnp.float32)
    return acc


def dispatch_rows(placed_rows, source, n_exp, capacity, n_core):
    core = lax.axis_index("core")
    width = source.shape[1]
    share = width // n_core
    mine = lax.dynamic_slice_in_dim(source, core * share, share, 1)
    sent = jnp.dot(placed_rows, mine, preferred_element_type=jnp.float32).astype(jnp.bfloat16)
    got = lax.all_to_all(
        sent.reshape(n_exp, capacity, share), "exp", split_axis=0, concat_axis=0, tiled=True
    ).reshape(n_exp * capacity, share)
    other = lax.ppermute(got, "core", [(j, (j + 1) % n_core) for j in range(n_core)])
    pair = jnp.stack([got, other])
    return jnp.concatenate([pick(pair, core, 0), pick(pair, 1 - core, 0)], axis=1)


def local(tokens, expert_ids, gate_values, grad_out, w_up, w_down):
    n_z = lax.axis_size("z")
    n_core = lax.axis_size("core")
    n_rep = n_z * n_core
    n_exp = lax.axis_size("exp")
    tok_count, width = tokens.shape
    top_k = expert_ids.shape[1]
    pair_count = tok_count * top_k
    capacity = max(2, min(tok_count, 2 * tok_count * top_k // n_exp))
    cols = width // n_rep
    up_weight = w_up[0]
    down_weight = w_down[0]
    ff_local = up_weight.shape[1]
    down_perm = (
        down_weight.reshape(ff_local, n_z, n_core, cols).transpose(0, 2, 1, 3).reshape(ff_local, width)
    )
    up_perm = up_weight.reshape(n_z, n_core, cols, ff_local).transpose(1, 0, 2, 3).reshape(width, ff_local)
    grad_rows = (gate_values[:, :, None] * grad_out[:, None, :].astype(jnp.float32)).astype(
        jnp.bfloat16
    )
    grad_rows = grad_rows.reshape(pair_count, width)
    placed, counts = plan_slots(expert_ids, n_exp, capacity)
    summed = placed.reshape(n_exp * capacity, tok_count, top_k).sum(axis=2)
    count_parts = jnp.stack([counts // 16, counts % 16], axis=1).astype(jnp.bfloat16)
    got_counts = lax.all_to_all(count_parts, "exp", split_axis=0, concat_axis=0, tiled=True)
    count_values = got_counts[:, 0].astype(jnp.float32) * 16.0 + got_counts[:, 1].astype(
        jnp.float32
    )
    slot_mask = jnp.arange(capacity, dtype=jnp.float32)[None, :] < count_values[:, None]
    live_mask = slot_mask.reshape(-1)
    rows_in = dispatch_rows(summed, tokens, n_exp, capacity, n_core)
    rows_grad = dispatch_rows(placed, grad_rows, n_exp, capacity, n_core)
    out_part, dx_part, grad_up_e, grad_down_e = expert_math(
        rows_in, rows_grad, live_mask, up_weight, down_weight, up_perm, down_perm
    )
    summed_out = reduce_over_rep(out_part.astype(jnp.bfloat16), n_z, n_core, cols)
    summed_dx = reduce_over_rep(dx_part.astype(jnp.bfloat16), n_z, n_core, cols)
    both = jnp.concatenate([summed_out, summed_dx], axis=1).astype(jnp.bfloat16)
    back_both = lax.all_to_all(
        both.reshape(n_exp, capacity, 2 * cols), "exp", split_axis=0, concat_axis=0, tiled=True
    ).reshape(n_exp * capacity, 2 * cols)
    back_out = back_both[:, :cols]
    back_dx = back_both[:, cols:]
    pair_out = jnp.einsum(
        "st,sd->td",
        placed,
        back_out,
        preferred_element_type=jnp.float32,
    )
    pair_dx = jnp.einsum(
        "st,sd->td",
        placed,
        back_dx,
        preferred_element_type=jnp.float32,
    )
    mixed = jnp.sum(gate_values[:, :, None] * pair_out.reshape(tok_count, top_k, cols), axis=1)
    grad_tokens = jnp.sum(pair_dx.reshape(tok_count, top_k, cols), axis=1)
    return (
        mixed.astype(jnp.bfloat16),
        grad_tokens.astype(jnp.bfloat16),
        grad_up_e.astype(jnp.bfloat16)[None],
        grad_down_e.astype(jnp.bfloat16)[None],
    )


def solution(mesh):
    n_rep, n_exp = mesh.devices.shape
    n_core = 2
    mesh3 = Mesh(mesh.devices.reshape(n_rep // n_core, n_core, n_exp), ("z", "core", "exp"))
    rep = ("z", "core")
    return jax.shard_map(
        local,
        mesh=mesh3,
        in_specs=(
            P("exp", None),
            P("exp", None),
            P("exp", None),
            P("exp", None),
            P("exp", None, rep),
            P("exp", rep, None),
        ),
        out_specs=(P("exp", rep), P("exp", rep), P("exp", None, rep), P("exp", rep, None)),
        check_vma=False,
    )
```

```python
import jax
import jax.numpy as jnp
from jax import lax
from jax.sharding import Mesh, PartitionSpec as P


def plan_slots(routed, experts, capacity):
    flat_ids = routed.reshape(-1)
    onehot = (flat_ids[:, None] == jnp.arange(experts, dtype=jnp.int32)[None, :]).astype(jnp.int32)
    before = jnp.cumsum(onehot, axis=0) - onehot
    position = jnp.sum(before * onehot, axis=1)
    counts = jnp.sum(onehot, axis=0)
    slotting_labels = flat_ids * capacity + position
    placed = (
        slotting_labels[None, :] == jnp.arange(experts * capacity, dtype=jnp.int32)[:, None]
    ).astype(jnp.bfloat16)
    return (placed, counts)


def expert_math(rows_in, rows_grad, live_mask, up_weight, down_weight, up_perm, down_perm):
    preact = jnp.dot(rows_in, up_weight, preferred_element_type=jnp.float32)
    sigmoid_val = jax.nn.sigmoid(preact)
    keep = live_mask[:, None]
    hidden_units = jnp.where(keep, preact * sigmoid_val, 0.0).astype(jnp.bfloat16)
    out_part = jnp.dot(hidden_units, down_perm, preferred_element_type=jnp.float32)
    grad_hidden = lax.dot_general(
        rows_grad, down_weight, (((1,), (1,)), ((), ())), preferred_element_type=jnp.float32
    )
    slope = sigmoid_val * (1.0 + preact * (1.0 - sigmoid_val))
    gradient_before_activation = jnp.where(keep, grad_hidden * slope, 0.0).astype(jnp.bfloat16)
    dx_part = lax.dot_general(
        gradient_before_activation,
        up_perm,
        (((1,), (1,)), ((), ())),
        preferred_element_type=jnp.float32,
    )
    grad_down_e = lax.dot_general(
        hidden_units, rows_grad, (((0,), (0,)), ((), ())), preferred_element_type=jnp.float32
    )
    grad_up_e = lax.dot_general(
        rows_in,
        gradient_before_activation,
        (((0,), (0,)), ((), ())),
        preferred_element_type=jnp.float32,
    )
    return (out_part, dx_part, grad_up_e, grad_down_e)


def pick(stacked, index, axis):
    return lax.dynamic_index_in_dim(stacked, index, axis=axis, keepdims=False)


def reduce_over_rep(part, n_z, n_core, cols):
    slots = part.shape[0]
    halves = part.reshape(slots, n_core, n_z * cols)
    got = lax.ppermute(halves[:, 1], "core", [(j, (j + 1) % n_core) for j in range(n_core)])
    pair_sum = (halves[:, 0].astype(jnp.float32) + got.astype(jnp.float32)).astype(jnp.bfloat16)
    blocks = pair_sum.reshape(slots, n_z, cols)
    acc = blocks[:, 0].astype(jnp.float32)
    for k in range(1, n_z):
        moved = lax.ppermute(blocks[:, k], "z", [(j, (j + k) % n_z) for j in range(n_z)])
        acc = acc + moved.astype(jnp.float32)
    return acc


def dispatch_rows(placed_rows, source, n_exp, capacity, n_core):
    core = lax.axis_index("core")
    width = source.shape[1]
    share = width // n_core
    mine = lax.dynamic_slice_in_dim(source, core * share, share, 1)
    sent = jnp.dot(placed_rows, mine, preferred_element_type=jnp.float32).astype(jnp.bfloat16)
    got = lax.all_to_all(
        sent.reshape(n_exp, capacity, share), "exp", split_axis=0, concat_axis=0, tiled=True
    ).reshape(n_exp * capacity, share)
    other = lax.ppermute(got, "core", [(j, (j + 1) % n_core) for j in range(n_core)])
    pair = jnp.stack([got, other])
    return jnp.concatenate([pick(pair, core, 0), pick(pair, 1 - core, 0)], axis=1)


def local(tokens, expert_ids, gate_values, grad_out, w_up, w_down):
    n_z = lax.axis_size("z")
    n_core = lax.axis_size("core")
    n_rep = n_z * n_core
    n_exp = lax.axis_size("exp")
    tok_count, width = tokens.shape
    top_k = expert_ids.shape[1]
    pair_count = tok_count * top_k
    capacity = max(2, min(tok_count, 2 * tok_count * top_k // n_exp))
    cols = width // n_rep
    up_weight = w_up[0]
    down_weight = w_down[0]
    ff_local = up_weight.shape[1]
    zi = lax.axis_index("z")
    core = lax.axis_index("core")
    down_blocks = jnp.roll(down_weight.reshape(ff_local, n_z, n_core, cols), (-zi, -core), (1, 2))
    down_perm = down_blocks.transpose(0, 2, 1, 3).reshape(ff_local, width)
    up_blocks = jnp.roll(up_weight.reshape(n_z, n_core, cols, ff_local), (-zi, -core), (0, 1))
    up_perm = up_blocks.transpose(1, 0, 2, 3).reshape(width, ff_local)
    grad_rows = (gate_values[:, :, None] * grad_out[:, None, :].astype(jnp.float32)).astype(
        jnp.bfloat16
    )
    grad_rows = grad_rows.reshape(pair_count, width)
    placed, counts = plan_slots(expert_ids, n_exp, capacity)
    summed = placed.reshape(n_exp * capacity, tok_count, top_k).sum(axis=2)
    count_parts = jnp.stack([counts // 16, counts % 16], axis=1).astype(jnp.bfloat16)
    got_counts = lax.all_to_all(count_parts, "exp", split_axis=0, concat_axis=0, tiled=True)
    count_values = got_counts[:, 0].astype(jnp.float32) * 16.0 + got_counts[:, 1].astype(
        jnp.float32
    )
    slot_mask = jnp.arange(capacity, dtype=jnp.float32)[None, :] < count_values[:, None]
    live_mask = slot_mask.reshape(-1)
    rows_in = dispatch_rows(summed, tokens, n_exp, capacity, n_core)
    rows_grad = dispatch_rows(placed, grad_rows, n_exp, capacity, n_core)
    out_part, dx_part, grad_up_e, grad_down_e = expert_math(
        rows_in, rows_grad, live_mask, up_weight, down_weight, up_perm, down_perm
    )
    parts = jnp.stack([out_part, dx_part], axis=1).astype(jnp.bfloat16)
    both = reduce_over_rep(parts.reshape(n_exp * capacity * 2, width), n_z, n_core, cols)
    both = both.reshape(n_exp * capacity, 2 * cols).astype(jnp.bfloat16)
    back_both = lax.all_to_all(
        both.reshape(n_exp, capacity, 2 * cols), "exp", split_axis=0, concat_axis=0, tiled=True
    ).reshape(n_exp * capacity, 2 * cols)
    back_out = back_both[:, :cols]
    back_dx = back_both[:, cols:]
    pair_out = jnp.einsum(
        "st,sd->td",
        placed,
        back_out,
        preferred_element_type=jnp.float32,
    )
    pair_dx = jnp.einsum(
        "st,sd->td",
        placed,
        back_dx,
        preferred_element_type=jnp.float32,
    )
    mixed = jnp.sum(gate_values[:, :, None] * pair_out.reshape(tok_count, top_k, cols), axis=1)
    grad_tokens = jnp.sum(pair_dx.reshape(tok_count, top_k, cols), axis=1)
    return (
        mixed.astype(jnp.bfloat16),
        grad_tokens.astype(jnp.bfloat16),
        grad_up_e.astype(jnp.bfloat16)[None],
        grad_down_e.astype(jnp.bfloat16)[None],
    )


def solution(mesh):
    n_rep, n_exp = mesh.devices.shape
    n_core = 2
    mesh3 = Mesh(mesh.devices.reshape(n_rep // n_core, n_core, n_exp), ("z", "core", "exp"))
    rep = ("z", "core")
    return jax.shard_map(
        local,
        mesh=mesh3,
        in_specs=(
            P("exp", None),
            P("exp", None),
            P("exp", None),
            P("exp", None),
            P("exp", None, rep),
            P("exp", rep, None),
        ),
        out_specs=(P("exp", rep), P("exp", rep), P("exp", None, rep), P("exp", rep, None)),
        check_vma=False,
    )
```

```python
import jax
import jax.numpy as jnp
from jax import lax
from jax.sharding import Mesh, PartitionSpec as P


def plan_slots(routed, experts, capacity):
    flat_ids = routed.reshape(-1)
    onehot = (flat_ids[:, None] == jnp.arange(experts, dtype=jnp.int32)[None, :]).astype(jnp.int32)
    before = jnp.cumsum(onehot, axis=0) - onehot
    position = jnp.sum(before * onehot, axis=1)
    counts = jnp.sum(onehot, axis=0)
    slotting_labels = flat_ids * capacity + position
    placed = (
        slotting_labels[None, :] == jnp.arange(experts * capacity, dtype=jnp.int32)[:, None]
    ).astype(jnp.bfloat16)
    return (placed, counts)


def expert_math(rows_in, rows_grad, up_weight, down_weight, up_perm, down_perm):
    preact = jnp.dot(rows_in, up_weight, preferred_element_type=jnp.float32)
    sigmoid_val = jax.nn.sigmoid(preact)
    hidden_units = (preact * sigmoid_val).astype(jnp.bfloat16)
    out_part = jnp.dot(hidden_units, down_perm, preferred_element_type=jnp.float32)
    grad_hidden = lax.dot_general(
        rows_grad, down_weight, (((1,), (1,)), ((), ())), preferred_element_type=jnp.float32
    )
    slope = sigmoid_val * (1.0 + preact * (1.0 - sigmoid_val))
    gradient_before_activation = (grad_hidden * slope).astype(jnp.bfloat16)
    dx_part = lax.dot_general(
        gradient_before_activation,
        up_perm,
        (((1,), (1,)), ((), ())),
        preferred_element_type=jnp.float32,
    )
    grad_down_e = lax.dot_general(
        hidden_units, rows_grad, (((0,), (0,)), ((), ())), preferred_element_type=jnp.float32
    )
    grad_up_e = lax.dot_general(
        rows_in,
        gradient_before_activation,
        (((0,), (0,)), ((), ())),
        preferred_element_type=jnp.float32,
    )
    return (out_part, dx_part, grad_up_e, grad_down_e)


def pick(stacked, index, axis):
    return lax.dynamic_index_in_dim(stacked, index, axis=axis, keepdims=False)


def reduce_over_rep(parts, n_z, n_core, cols):
    share = n_z * cols
    got = lax.ppermute(
        jnp.concatenate([p[:, share:] for p in parts], axis=0),
        "core",
        [(j, (j + 1) % n_core) for j in range(n_core)],
    )
    own = jnp.concatenate([p[:, :share] for p in parts], axis=0)
    pair_sum = (own.astype(jnp.float32) + got.astype(jnp.float32)).astype(jnp.bfloat16)
    acc = pair_sum[:, :cols].astype(jnp.float32)
    for k in range(1, n_z):
        piece = pair_sum[:, k * cols : (k + 1) * cols]
        moved = lax.ppermute(piece, "z", [(j, (j + k) % n_z) for j in range(n_z)])
        acc = acc + moved.astype(jnp.float32)
    return acc


def dispatch_rows(placements, sources, n_exp, capacity, n_core):
    core = lax.axis_index("core")
    width = sources[0].shape[1]
    share = width // n_core
    sent = jnp.concatenate(
        [
            jnp.dot(
                placed_rows,
                lax.dynamic_slice_in_dim(source, core * share, share, 1),
                preferred_element_type=jnp.float32,
            ).astype(jnp.bfloat16)
            for placed_rows, source in zip(placements, sources)
        ],
        axis=1,
    )
    got = lax.all_to_all(
        sent.reshape(n_exp, capacity, sent.shape[1]), "exp", split_axis=0, concat_axis=0, tiled=True
    ).reshape(n_exp * capacity, sent.shape[1])
    other = lax.ppermute(got, "core", [(j, (j + 1) % n_core) for j in range(n_core)])
    pair = jnp.stack([got, other])
    first, second = pick(pair, core, 0), pick(pair, 1 - core, 0)
    return [
        jnp.concatenate([first[:, i * share : (i + 1) * share], second[:, i * share : (i + 1) * share]], axis=1)
        for i in range(len(sources))
    ]


def local(tokens, expert_ids, gate_values, grad_out, w_up, w_down):
    n_z = lax.axis_size("z")
    n_core = lax.axis_size("core")
    n_rep = n_z * n_core
    n_exp = lax.axis_size("exp")
    tok_count, width = tokens.shape
    top_k = expert_ids.shape[1]
    pair_count = tok_count * top_k
    capacity = max(2, min(tok_count, 2 * tok_count * top_k // n_exp))
    cols = width // n_rep
    up_weight = w_up[0]
    down_weight = w_down[0]
    ff_local = up_weight.shape[1]
    zi = lax.axis_index("z")
    core = lax.axis_index("core")
    down_blocks = jnp.roll(down_weight.reshape(ff_local, n_z, n_core, cols), (-zi, -core), (1, 2))
    down_perm = down_blocks.transpose(0, 2, 1, 3).reshape(ff_local, width)
    up_blocks = jnp.roll(up_weight.reshape(n_z, n_core, cols, ff_local), (-zi, -core), (0, 1))
    up_perm = up_blocks.transpose(1, 0, 2, 3).reshape(width, ff_local)
    grad_rows = (gate_values[:, :, None] * grad_out[:, None, :].astype(jnp.float32)).astype(
        jnp.bfloat16
    )
    grad_rows = grad_rows.reshape(pair_count, width)
    placed, counts = plan_slots(expert_ids, n_exp, capacity)
    summed = placed.reshape(n_exp * capacity, tok_count, top_k).sum(axis=2)
    rows_in, rows_grad = dispatch_rows((summed, placed), (tokens, grad_rows), n_exp, capacity, n_core)
    out_part, dx_part, grad_up_e, grad_down_e = expert_math(
        rows_in, rows_grad, up_weight, down_weight, up_perm, down_perm
    )
    acc = reduce_over_rep(
        (out_part.astype(jnp.bfloat16), dx_part.astype(jnp.bfloat16)), n_z, n_core, cols
    )
    slots = n_exp * capacity
    both = jnp.concatenate([acc[:slots], acc[slots:]], axis=1).astype(jnp.bfloat16)
    back_both = lax.all_to_all(
        both.reshape(n_exp, capacity, 2 * cols), "exp", split_axis=0, concat_axis=0, tiled=True
    ).reshape(n_exp * capacity, 2 * cols)
    back_out = back_both[:, :cols]
    back_dx = back_both[:, cols:]
    pair_out = jnp.einsum(
        "st,sd->td",
        placed,
        back_out,
        preferred_element_type=jnp.float32,
    )
    pair_dx = jnp.einsum(
        "st,sd->td",
        placed,
        back_dx,
        preferred_element_type=jnp.float32,
    )
    mixed = jnp.sum(gate_values[:, :, None] * pair_out.reshape(tok_count, top_k, cols), axis=1)
    grad_tokens = jnp.sum(pair_dx.reshape(tok_count, top_k, cols), axis=1)
    return (
        mixed.astype(jnp.bfloat16),
        grad_tokens.astype(jnp.bfloat16),
        grad_up_e.astype(jnp.bfloat16)[None],
        grad_down_e.astype(jnp.bfloat16)[None],
    )


def solution(mesh):
    n_rep, n_exp = mesh.devices.shape
    n_core = 2
    mesh3 = Mesh(mesh.devices.reshape(n_rep // n_core, n_core, n_exp), ("z", "core", "exp"))
    rep = ("z", "core")
    return jax.shard_map(
        local,
        mesh=mesh3,
        in_specs=(
            P("exp", None),
            P("exp", None),
            P("exp", None),
            P("exp", None),
            P("exp", None, rep),
            P("exp", rep, None),
        ),
        out_specs=(P("exp", rep), P("exp", rep), P("exp", None, rep), P("exp", rep, None)),
        check_vma=False,
    )
```

```python
import jax
import jax.numpy as jnp
from jax import lax
from jax.sharding import Mesh, PartitionSpec as P


def plan_slots(routed, experts, capacity):
    flat_ids = routed.reshape(-1)
    onehot = (flat_ids[:, None] == jnp.arange(experts, dtype=jnp.int32)[None, :]).astype(jnp.int32)
    before = jnp.cumsum(onehot, axis=0) - onehot
    position = jnp.sum(before * onehot, axis=1)
    counts = jnp.sum(onehot, axis=0)
    slotting_labels = flat_ids * capacity + position
    placed = (
        slotting_labels[None, :] == jnp.arange(experts * capacity, dtype=jnp.int32)[:, None]
    ).astype(jnp.bfloat16)
    return (placed, counts)


def expert_math(rows_in, rows_grad, up_weight, down_weight, up_perm, down_perm):
    preact = jnp.dot(rows_in, up_weight, preferred_element_type=jnp.float32)
    sigmoid_val = jax.nn.sigmoid(preact)
    hidden_units = (preact * sigmoid_val).astype(jnp.bfloat16)
    out_part = jnp.dot(hidden_units, down_perm, preferred_element_type=jnp.float32)
    grad_hidden = lax.dot_general(
        rows_grad, down_weight, (((1,), (1,)), ((), ())), preferred_element_type=jnp.float32
    )
    slope = sigmoid_val * (1.0 + preact * (1.0 - sigmoid_val))
    gradient_before_activation = (grad_hidden * slope).astype(jnp.bfloat16)
    dx_part = lax.dot_general(
        gradient_before_activation,
        up_perm,
        (((1,), (1,)), ((), ())),
        preferred_element_type=jnp.float32,
    )
    grad_down_e = lax.dot_general(
        hidden_units, rows_grad, (((0,), (0,)), ((), ())), preferred_element_type=jnp.float32
    )
    grad_up_e = lax.dot_general(
        rows_in,
        gradient_before_activation,
        (((0,), (0,)), ((), ())),
        preferred_element_type=jnp.float32,
    )
    return (out_part, dx_part, grad_up_e, grad_down_e)


def pick(stacked, index, axis):
    return lax.dynamic_index_in_dim(stacked, index, axis=axis, keepdims=False)


def reduce_over_rep(parts, n_z, n_core, cols):
    share = n_z * cols
    got = lax.ppermute(
        jnp.concatenate([p[:, share:] for p in parts], axis=0),
        "core",
        [(j, (j + 1) % n_core) for j in range(n_core)],
    )
    own = jnp.concatenate([p[:, :share] for p in parts], axis=0)
    pair_sum = (own.astype(jnp.float32) + got.astype(jnp.float32)).astype(jnp.bfloat16)
    block = [pair_sum[:, k * cols : (k + 1) * cols] for k in range(n_z)]
    acc = block[0].astype(jnp.float32)
    if n_z != 8:
        for k in range(1, n_z):
            moved = lax.ppermute(block[k], "z", [(j, (j + k) % n_z) for j in range(n_z)])
            acc = acc + moved.astype(jnp.float32)
        return acc

    def shift(x, k):
        return lax.ppermute(x, "z", [(j, (j + k) % n_z) for j in range(n_z)]).astype(jnp.float32)

    rows = pair_sum.shape[0]
    top = rows // 2
    near_up = shift(block[1], 1)
    near_down = shift(block[7], -1)
    via_up = shift(block[3], 1)
    via_down = shift(block[5], -1)
    far_up = shift(block[4][:top], 2)
    far_down = shift(block[4][top:], -2)
    zeros = jnp.zeros((rows - top, cols), jnp.float32)
    agg_up = block[2].astype(jnp.float32) + via_up + jnp.concatenate([far_up, zeros], axis=0)
    agg_down = block[6].astype(jnp.float32) + via_down + jnp.concatenate([zeros, far_down], axis=0)
    acc = acc + near_up + near_down
    acc = acc + shift(agg_up.astype(jnp.bfloat16), 2)
    acc = acc + shift(agg_down.astype(jnp.bfloat16), -2)
    return acc


def dispatch_rows(placements, sources, n_exp, capacity, n_core):
    core = lax.axis_index("core")
    width = sources[0].shape[1]
    share = width // n_core
    sent = jnp.concatenate(
        [
            jnp.dot(
                placed_rows,
                lax.dynamic_slice_in_dim(source, core * share, share, 1),
                preferred_element_type=jnp.float32,
            ).astype(jnp.bfloat16)
            for placed_rows, source in zip(placements, sources)
        ],
        axis=1,
    )
    got = lax.all_to_all(
        sent.reshape(n_exp, capacity, sent.shape[1]), "exp", split_axis=0, concat_axis=0, tiled=True
    ).reshape(n_exp * capacity, sent.shape[1])
    other = lax.ppermute(got, "core", [(j, (j + 1) % n_core) for j in range(n_core)])
    pair = jnp.stack([got, other])
    first, second = pick(pair, core, 0), pick(pair, 1 - core, 0)
    return [
        jnp.concatenate([first[:, i * share : (i + 1) * share], second[:, i * share : (i + 1) * share]], axis=1)
        for i in range(len(sources))
    ]


def local(tokens, expert_ids, gate_values, grad_out, w_up, w_down):
    n_z = lax.axis_size("z")
    n_core = lax.axis_size("core")
    n_rep = n_z * n_core
    n_exp = lax.axis_size("exp")
    tok_count, width = tokens.shape
    top_k = expert_ids.shape[1]
    pair_count = tok_count * top_k
    capacity = max(2, min(tok_count, 2 * tok_count * top_k // n_exp))
    cols = width // n_rep
    up_weight = w_up[0]
    down_weight = w_down[0]
    ff_local = up_weight.shape[1]
    zi = lax.axis_index("z")
    core = lax.axis_index("core")
    down_blocks = jnp.roll(down_weight.reshape(ff_local, n_z, n_core, cols), (-zi, -core), (1, 2))
    down_perm = down_blocks.transpose(0, 2, 1, 3).reshape(ff_local, width)
    up_blocks = jnp.roll(up_weight.reshape(n_z, n_core, cols, ff_local), (-zi, -core), (0, 1))
    up_perm = up_blocks.transpose(1, 0, 2, 3).reshape(width, ff_local)
    grad_rows = (gate_values[:, :, None] * grad_out[:, None, :].astype(jnp.float32)).astype(
        jnp.bfloat16
    )
    grad_rows = grad_rows.reshape(pair_count, width)
    placed, counts = plan_slots(expert_ids, n_exp, capacity)
    summed = placed.reshape(n_exp * capacity, tok_count, top_k).sum(axis=2)
    rows_in, rows_grad = dispatch_rows((summed, placed), (tokens, grad_rows), n_exp, capacity, n_core)
    out_part, dx_part, grad_up_e, grad_down_e = expert_math(
        rows_in, rows_grad, up_weight, down_weight, up_perm, down_perm
    )
    acc = reduce_over_rep(
        (out_part.astype(jnp.bfloat16), dx_part.astype(jnp.bfloat16)), n_z, n_core, cols
    )
    slots = n_exp * capacity
    both = jnp.concatenate([acc[:slots], acc[slots:]], axis=1).astype(jnp.bfloat16)
    back_both = lax.all_to_all(
        both.reshape(n_exp, capacity, 2 * cols), "exp", split_axis=0, concat_axis=0, tiled=True
    ).reshape(n_exp * capacity, 2 * cols)
    back_out = back_both[:, :cols]
    back_dx = back_both[:, cols:]
    pair_out = jnp.einsum(
        "st,sd->td",
        placed,
        back_out,
        preferred_element_type=jnp.float32,
    )
    pair_dx = jnp.einsum(
        "st,sd->td",
        placed,
        back_dx,
        preferred_element_type=jnp.float32,
    )
    mixed = jnp.sum(gate_values[:, :, None] * pair_out.reshape(tok_count, top_k, cols), axis=1)
    grad_tokens = jnp.sum(pair_dx.reshape(tok_count, top_k, cols), axis=1)
    return (
        mixed.astype(jnp.bfloat16),
        grad_tokens.astype(jnp.bfloat16),
        grad_up_e.astype(jnp.bfloat16)[None],
        grad_down_e.astype(jnp.bfloat16)[None],
    )


def solution(mesh):
    n_rep, n_exp = mesh.devices.shape
    n_core = 2
    mesh3 = Mesh(mesh.devices.reshape(n_rep // n_core, n_core, n_exp), ("z", "core", "exp"))
    rep = ("z", "core")
    return jax.shard_map(
        local,
        mesh=mesh3,
        in_specs=(
            P("exp", None),
            P("exp", None),
            P("exp", None),
            P("exp", None),
            P("exp", None, rep),
            P("exp", rep, None),
        ),
        out_specs=(P("exp", rep), P("exp", rep), P("exp", None, rep), P("exp", rep, None)),
        check_vma=False,
    )
```

```python
import jax
import jax.numpy as jnp
from jax import lax
from jax.sharding import Mesh, PartitionSpec as P


def plan_slots(routed, experts, capacity):
    flat_ids = routed.reshape(-1)
    onehot = (flat_ids[:, None] == jnp.arange(experts, dtype=jnp.int32)[None, :]).astype(jnp.int32)
    before = jnp.cumsum(onehot, axis=0) - onehot
    position = jnp.sum(before * onehot, axis=1)
    counts = jnp.sum(onehot, axis=0)
    slotting_labels = flat_ids * capacity + position
    placed = (
        slotting_labels[None, :] == jnp.arange(experts * capacity, dtype=jnp.int32)[:, None]
    ).astype(jnp.bfloat16)
    return (placed, counts)


def expert_math(rows_in, rows_grad, up_weight, down_weight, up_perm, down_perm):
    preact = jnp.dot(rows_in, up_weight, preferred_element_type=jnp.float32)
    sigmoid_val = jax.nn.sigmoid(preact)
    hidden_units = (preact * sigmoid_val).astype(jnp.bfloat16)
    out_part = jnp.dot(hidden_units, down_perm, preferred_element_type=jnp.float32)
    grad_hidden = lax.dot_general(
        rows_grad, down_weight, (((1,), (1,)), ((), ())), preferred_element_type=jnp.float32
    )
    slope = sigmoid_val * (1.0 + preact * (1.0 - sigmoid_val))
    gradient_before_activation = (grad_hidden * slope).astype(jnp.bfloat16)
    dx_part = lax.dot_general(
        gradient_before_activation,
        up_perm,
        (((1,), (1,)), ((), ())),
        preferred_element_type=jnp.float32,
    )
    grad_down_e = lax.dot_general(
        hidden_units, rows_grad, (((0,), (0,)), ((), ())), preferred_element_type=jnp.float32
    )
    grad_up_e = lax.dot_general(
        rows_in,
        gradient_before_activation,
        (((0,), (0,)), ((), ())),
        preferred_element_type=jnp.float32,
    )
    return (out_part, dx_part, grad_up_e, grad_down_e)


def pick(stacked, index, axis):
    return lax.dynamic_index_in_dim(stacked, index, axis=axis, keepdims=False)


def reduce_over_rep(parts, n_z, n_core, cols):
    share = n_z * cols
    got = lax.ppermute(
        jnp.concatenate([p[:, share:] for p in parts], axis=0),
        "core",
        [(j, (j + 1) % n_core) for j in range(n_core)],
    )
    own = jnp.concatenate([p[:, :share] for p in parts], axis=0)
    pair_sum = (own.astype(jnp.float32) + got.astype(jnp.float32)).astype(jnp.bfloat16)
    block = [pair_sum[:, k * cols : (k + 1) * cols] for k in range(n_z)]
    acc = block[0].astype(jnp.float32)
    if n_z != 8:
        for k in range(1, n_z):
            moved = lax.ppermute(block[k], "z", [(j, (j + k) % n_z) for j in range(n_z)])
            acc = acc + moved.astype(jnp.float32)
        return acc

    def shift(x, k):
        return lax.ppermute(x, "z", [(j, (j + k) % n_z) for j in range(n_z)]).astype(jnp.float32)

    rows = pair_sum.shape[0]
    top = rows // 2
    near_up = shift(block[1], 1)
    near_down = shift(block[7], -1)
    via_up = shift(block[3], 1)
    via_down = shift(block[5], -1)
    far_up = shift(block[4][:top], 2)
    far_down = shift(block[4][top:], -2)
    zeros = jnp.zeros((rows - top, cols), jnp.float32)
    agg_up = block[2].astype(jnp.float32) + via_up + jnp.concatenate([far_up, zeros], axis=0)
    agg_down = block[6].astype(jnp.float32) + via_down + jnp.concatenate([zeros, far_down], axis=0)
    acc = acc + near_up + near_down
    acc = acc + shift(agg_up.astype(jnp.bfloat16), 2)
    acc = acc + shift(agg_down.astype(jnp.bfloat16), -2)
    return acc


def dispatch_rows(placements, sources, n_exp, capacity, n_core):
    core = lax.axis_index("core")
    share = sources[0].shape[1]
    sent = jnp.concatenate(
        [
            jnp.dot(placed_rows, source, preferred_element_type=jnp.float32).astype(jnp.bfloat16)
            for placed_rows, source in zip(placements, sources)
        ],
        axis=1,
    )
    got = lax.all_to_all(
        sent.reshape(n_exp, capacity, sent.shape[1]), "exp", split_axis=0, concat_axis=0, tiled=True
    ).reshape(n_exp * capacity, sent.shape[1])
    other = lax.ppermute(got, "core", [(j, (j + 1) % n_core) for j in range(n_core)])
    pair = jnp.stack([got, other])
    first, second = pick(pair, core, 0), pick(pair, 1 - core, 0)
    return [
        jnp.concatenate([first[:, i * share : (i + 1) * share], second[:, i * share : (i + 1) * share]], axis=1)
        for i in range(len(sources))
    ]


def local(tokens, expert_ids, gate_values, grad_out, w_up, w_down):
    n_z = lax.axis_size("z")
    n_core = lax.axis_size("core")
    n_rep = n_z * n_core
    n_exp = lax.axis_size("exp")
    tok_count, width = tokens.shape
    top_k = expert_ids.shape[1]
    pair_count = tok_count * top_k
    capacity = max(2, min(tok_count, 2 * tok_count * top_k // n_exp))
    cols = width // n_rep
    up_weight = w_up[0]
    down_weight = w_down[0]
    ff_local = up_weight.shape[1]
    zi = lax.axis_index("z")
    core = lax.axis_index("core")
    down_blocks = jnp.roll(down_weight.reshape(ff_local, n_z, n_core, cols), (-zi, -core), (1, 2))
    down_perm = down_blocks.transpose(0, 2, 1, 3).reshape(ff_local, width)
    up_blocks = jnp.roll(up_weight.reshape(n_z, n_core, cols, ff_local), (-zi, -core), (0, 1))
    up_perm = up_blocks.transpose(1, 0, 2, 3).reshape(width, ff_local)
    share = width // n_core
    tok_half = lax.dynamic_slice_in_dim(tokens, core * share, share, 1)
    grad_half = lax.dynamic_slice_in_dim(grad_out, core * share, share, 1)
    grad_rows = (gate_values[:, :, None] * grad_half[:, None, :].astype(jnp.float32)).astype(
        jnp.bfloat16
    )
    grad_rows = grad_rows.reshape(pair_count, share)
    placed, _ = plan_slots(expert_ids, n_exp, capacity)
    summed = placed.reshape(n_exp * capacity, tok_count, top_k).sum(axis=2)
    n_chunks = 2 if capacity % 2 == 0 else 1
    chunk_cap = capacity // n_chunks
    slots = n_exp * chunk_cap
    placed_blocks = placed.reshape(n_exp, capacity, pair_count)
    summed_blocks = summed.reshape(n_exp, capacity, tok_count)
    grad_up_e = grad_down_e = pair_out = pair_dx = 0.0
    for c in range(n_chunks):
        span = slice(c * chunk_cap, (c + 1) * chunk_cap)
        placed_c = placed_blocks[:, span].reshape(slots, pair_count)
        summed_c = summed_blocks[:, span].reshape(slots, tok_count)
        rows_in, rows_grad = dispatch_rows(
            (summed_c, placed_c), (tok_half, grad_rows), n_exp, chunk_cap, n_core
        )
        out_part, dx_part, grad_up_c, grad_down_c = expert_math(
            rows_in, rows_grad, up_weight, down_weight, up_perm, down_perm
        )
        grad_up_e = grad_up_e + grad_up_c
        grad_down_e = grad_down_e + grad_down_c
        acc = reduce_over_rep(
            (out_part.astype(jnp.bfloat16), dx_part.astype(jnp.bfloat16)), n_z, n_core, cols
        )
        both = jnp.concatenate([acc[:slots], acc[slots:]], axis=1).astype(jnp.bfloat16)
        back_both = lax.all_to_all(
            both.reshape(n_exp, chunk_cap, 2 * cols), "exp", split_axis=0, concat_axis=0, tiled=True
        ).reshape(slots, 2 * cols)
        pair_out = pair_out + jnp.einsum(
            "st,sd->td", placed_c, back_both[:, :cols], preferred_element_type=jnp.float32
        )
        pair_dx = pair_dx + jnp.einsum(
            "st,sd->td", placed_c, back_both[:, cols:], preferred_element_type=jnp.float32
        )
    mixed = jnp.sum(gate_values[:, :, None] * pair_out.reshape(tok_count, top_k, cols), axis=1)
    grad_tokens = jnp.sum(pair_dx.reshape(tok_count, top_k, cols), axis=1)
    return (
        mixed.astype(jnp.bfloat16),
        grad_tokens.astype(jnp.bfloat16),
        grad_up_e.astype(jnp.bfloat16)[None],
        grad_down_e.astype(jnp.bfloat16)[None],
    )


def solution(mesh):
    n_rep, n_exp = mesh.devices.shape
    n_core = 2
    mesh3 = Mesh(mesh.devices.reshape(n_rep // n_core, n_core, n_exp), ("z", "core", "exp"))
    rep = ("z", "core")
    return jax.shard_map(
        local,
        mesh=mesh3,
        in_specs=(
            P("exp", None),
            P("exp", None),
            P("exp", None),
            P("exp", None),
            P("exp", None, rep),
            P("exp", rep, None),
        ),
        out_specs=(P("exp", rep), P("exp", rep), P("exp", None, rep), P("exp", rep, None)),
        check_vma=False,
    )
```

```python
import jax
import jax.numpy as jnp
from jax import lax
from jax.sharding import Mesh, PartitionSpec as P


def plan_slots(routed, experts, capacity):
    flat_ids = routed.reshape(-1)
    onehot = (flat_ids[:, None] == jnp.arange(experts, dtype=jnp.int32)[None, :]).astype(jnp.int32)
    before = jnp.cumsum(onehot, axis=0) - onehot
    position = jnp.sum(before * onehot, axis=1)
    counts = jnp.sum(onehot, axis=0)
    slotting_labels = flat_ids * capacity + position
    placed = (
        slotting_labels[None, :] == jnp.arange(experts * capacity, dtype=jnp.int32)[:, None]
    ).astype(jnp.bfloat16)
    return (placed, counts)


def expert_math(rows_in, rows_grad, up_weight, down_weight, up_perm, down_perm):
    preact = jnp.dot(rows_in, up_weight, preferred_element_type=jnp.float32)
    sigmoid_val = jax.nn.sigmoid(preact)
    hidden_units = (preact * sigmoid_val).astype(jnp.bfloat16)
    out_part = jnp.dot(hidden_units, down_perm, preferred_element_type=jnp.float32)
    grad_hidden = lax.dot_general(
        rows_grad, down_weight, (((1,), (1,)), ((), ())), preferred_element_type=jnp.float32
    )
    slope = sigmoid_val * (1.0 + preact * (1.0 - sigmoid_val))
    gradient_before_activation = (grad_hidden * slope).astype(jnp.bfloat16)
    dx_part = lax.dot_general(
        gradient_before_activation,
        up_perm,
        (((1,), (1,)), ((), ())),
        preferred_element_type=jnp.float32,
    )
    grad_down_e = lax.dot_general(
        hidden_units, rows_grad, (((0,), (0,)), ((), ())), preferred_element_type=jnp.float32
    )
    grad_up_e = lax.dot_general(
        rows_in,
        gradient_before_activation,
        (((0,), (0,)), ((), ())),
        preferred_element_type=jnp.float32,
    )
    return (out_part, dx_part, grad_up_e, grad_down_e)


def pick(stacked, index, axis):
    return lax.dynamic_index_in_dim(stacked, index, axis=axis, keepdims=False)


def reduce_over_rep(parts, n_z, n_core, cols):
    share = n_z * cols
    got = lax.ppermute(
        jnp.concatenate([p[:, share:] for p in parts], axis=0),
        "core",
        [(j, (j + 1) % n_core) for j in range(n_core)],
    )
    own = jnp.concatenate([p[:, :share] for p in parts], axis=0)
    pair_sum = (own.astype(jnp.float32) + got.astype(jnp.float32)).astype(jnp.bfloat16)
    block = [pair_sum[:, k * cols : (k + 1) * cols] for k in range(n_z)]
    acc = block[0].astype(jnp.float32)
    if n_z != 8:
        for k in range(1, n_z):
            moved = lax.ppermute(block[k], "z", [(j, (j + k) % n_z) for j in range(n_z)])
            acc = acc + moved.astype(jnp.float32)
        return acc

    def shift(x, k):
        return lax.ppermute(x, "z", [(j, (j + k) % n_z) for j in range(n_z)]).astype(jnp.float32)

    rows = pair_sum.shape[0]
    top = rows // 2
    near_up = shift(block[1], 1)
    near_down = shift(block[7], -1)
    via_up = shift(block[3], 1)
    via_down = shift(block[5], -1)
    far_up = shift(block[4][:top], 2)
    far_down = shift(block[4][top:], -2)
    zeros = jnp.zeros((rows - top, cols), jnp.float32)
    agg_up = block[2].astype(jnp.float32) + via_up + jnp.concatenate([far_up, zeros], axis=0)
    agg_down = block[6].astype(jnp.float32) + via_down + jnp.concatenate([zeros, far_down], axis=0)
    acc = acc + near_up + near_down
    acc = acc + shift(agg_up.astype(jnp.bfloat16), 2)
    acc = acc + shift(agg_down.astype(jnp.bfloat16), -2)
    return acc


def dispatch_rows(placements, sources, n_exp, capacity, n_core):
    core = lax.axis_index("core")
    share = sources[0].shape[1]
    sent = jnp.concatenate(
        [
            jnp.dot(placed_rows, source, preferred_element_type=jnp.float32).astype(jnp.bfloat16)
            for placed_rows, source in zip(placements, sources)
        ],
        axis=1,
    )
    got = lax.all_to_all(
        sent.reshape(n_exp, capacity, sent.shape[1]), "exp", split_axis=0, concat_axis=0, tiled=True
    ).reshape(n_exp * capacity, sent.shape[1])
    other = lax.ppermute(got, "core", [(j, (j + 1) % n_core) for j in range(n_core)])
    pair = jnp.stack([got, other])
    first, second = pick(pair, core, 0), pick(pair, 1 - core, 0)
    return [
        jnp.concatenate([first[:, i * share : (i + 1) * share], second[:, i * share : (i + 1) * share]], axis=1)
        for i in range(len(sources))
    ]


def local(tokens, expert_ids, gate_values, grad_out, w_up, w_down):
    n_z = lax.axis_size("z")
    n_core = lax.axis_size("core")
    n_rep = n_z * n_core
    n_exp = lax.axis_size("exp")
    tok_count, width = tokens.shape
    top_k = expert_ids.shape[1]
    pair_count = tok_count * top_k
    capacity = max(2, min(tok_count, 2 * tok_count * top_k // n_exp))
    cols = width // n_rep
    up_weight = w_up[0]
    down_weight = w_down[0]
    ff_local = up_weight.shape[1]
    zi = lax.axis_index("z")
    core = lax.axis_index("core")
    down_blocks = jnp.roll(down_weight.reshape(ff_local, n_z, n_core, cols), (-zi, -core), (1, 2))
    down_perm = down_blocks.transpose(0, 2, 1, 3).reshape(ff_local, width)
    up_blocks = jnp.roll(up_weight.reshape(n_z, n_core, cols, ff_local), (-zi, -core), (0, 1))
    up_perm = up_blocks.transpose(1, 0, 2, 3).reshape(width, ff_local)
    share = width // n_core
    tok_half = lax.dynamic_slice_in_dim(tokens, core * share, share, 1)
    grad_half = lax.dynamic_slice_in_dim(grad_out, core * share, share, 1)
    grad_rows = (gate_values[:, :, None] * grad_half[:, None, :].astype(jnp.float32)).astype(
        jnp.bfloat16
    )
    grad_rows = grad_rows.reshape(pair_count, share)
    placed, _ = plan_slots(expert_ids, n_exp, capacity)
    summed = placed.reshape(n_exp * capacity, tok_count, top_k).sum(axis=2)
    rows_in, rows_grad = dispatch_rows((summed, placed), (tok_half, grad_rows), n_exp, capacity, n_core)
    out_part, dx_part, grad_up_e, grad_down_e = expert_math(
        rows_in, rows_grad, up_weight, down_weight, up_perm, down_perm
    )
    acc = reduce_over_rep(
        (out_part.astype(jnp.bfloat16), dx_part.astype(jnp.bfloat16)), n_z, n_core, cols
    )
    slots = n_exp * capacity
    both = jnp.concatenate([acc[:slots], acc[slots:]], axis=1).astype(jnp.bfloat16)
    back_both = lax.all_to_all(
        both.reshape(n_exp, capacity, 2 * cols), "exp", split_axis=0, concat_axis=0, tiled=True
    ).reshape(n_exp * capacity, 2 * cols)
    back_out = back_both[:, :cols]
    back_dx = back_both[:, cols:]
    pair_out = jnp.einsum(
        "st,sd->td",
        placed,
        back_out,
        preferred_element_type=jnp.float32,
    )
    pair_dx = jnp.einsum(
        "st,sd->td",
        placed,
        back_dx,
        preferred_element_type=jnp.float32,
    )
    mixed = jnp.sum(gate_values[:, :, None] * pair_out.reshape(tok_count, top_k, cols), axis=1)
    grad_tokens = jnp.sum(pair_dx.reshape(tok_count, top_k, cols), axis=1)
    return (
        mixed.astype(jnp.bfloat16),
        grad_tokens.astype(jnp.bfloat16),
        grad_up_e.astype(jnp.bfloat16)[None],
        grad_down_e.astype(jnp.bfloat16)[None],
    )


def solution(mesh):
    n_rep, n_exp = mesh.devices.shape
    n_core = 2
    mesh3 = Mesh(mesh.devices.reshape(n_rep // n_core, n_core, n_exp), ("z", "core", "exp"))
    rep = ("z", "core")
    return jax.shard_map(
        local,
        mesh=mesh3,
        in_specs=(
            P("exp", None),
            P("exp", None),
            P("exp", None),
            P("exp", None),
            P("exp", None, rep),
            P("exp", rep, None),
        ),
        out_specs=(P("exp", rep), P("exp", rep), P("exp", None, rep), P("exp", rep, None)),
        check_vma=False,
    )
```

```python
import jax
import jax.numpy as jnp
from jax import lax
from jax.sharding import Mesh, PartitionSpec as P


def plan_slots(routed, experts, capacity):
    flat_ids = routed.reshape(-1)
    onehot = (flat_ids[:, None] == jnp.arange(experts, dtype=jnp.int32)[None, :]).astype(jnp.int32)
    before = jnp.cumsum(onehot, axis=0) - onehot
    position = jnp.sum(before * onehot, axis=1)
    counts = jnp.sum(onehot, axis=0)
    slotting_labels = flat_ids * capacity + position
    placed = (
        slotting_labels[None, :] == jnp.arange(experts * capacity, dtype=jnp.int32)[:, None]
    ).astype(jnp.bfloat16)
    return (placed, counts)


def expert_math(rows_in, rows_grad, up_weight, down_weight, up_perm, down_perm):
    preact = jnp.dot(rows_in, up_weight, preferred_element_type=jnp.float32)
    sigmoid_val = jax.nn.sigmoid(preact)
    hidden_units = (preact * sigmoid_val).astype(jnp.bfloat16)
    out_part = jnp.dot(hidden_units, down_perm, preferred_element_type=jnp.float32)
    grad_hidden = lax.dot_general(
        rows_grad, down_weight, (((1,), (1,)), ((), ())), preferred_element_type=jnp.float32
    )
    slope = sigmoid_val * (1.0 + preact * (1.0 - sigmoid_val))
    gradient_before_activation = (grad_hidden * slope).astype(jnp.bfloat16)
    dx_part = lax.dot_general(
        gradient_before_activation,
        up_perm,
        (((1,), (1,)), ((), ())),
        preferred_element_type=jnp.float32,
    )
    grad_down_e = lax.dot_general(
        hidden_units, rows_grad, (((0,), (0,)), ((), ())), preferred_element_type=jnp.float32
    )
    grad_up_e = lax.dot_general(
        rows_in,
        gradient_before_activation,
        (((0,), (0,)), ((), ())),
        preferred_element_type=jnp.float32,
    )
    return (out_part, dx_part, grad_up_e, grad_down_e)


def pick(stacked, index, axis):
    return lax.dynamic_index_in_dim(stacked, index, axis=axis, keepdims=False)


def reduce_over_rep(parts, n_z, n_core, cols):
    share = n_z * cols
    got = lax.ppermute(
        jnp.concatenate([p[:, share:] for p in parts], axis=0),
        "core",
        [(j, (j + 1) % n_core) for j in range(n_core)],
    )
    own = jnp.concatenate([p[:, :share] for p in parts], axis=0)
    pair_sum = (own.astype(jnp.float32) + got.astype(jnp.float32)).astype(jnp.bfloat16)
    block = [pair_sum[:, k * cols : (k + 1) * cols] for k in range(n_z)]
    acc = block[0].astype(jnp.float32)
    if n_z != 8:
        for k in range(1, n_z):
            moved = lax.ppermute(block[k], "z", [(j, (j + k) % n_z) for j in range(n_z)])
            acc = acc + moved.astype(jnp.float32)
        return acc

    def shift(x, k):
        return lax.ppermute(x, "z", [(j, (j + k) % n_z) for j in range(n_z)]).astype(jnp.float32)

    rows = pair_sum.shape[0]
    top = rows // 2
    up_pair = shift(jnp.concatenate([block[1], block[3]], axis=0), 1)
    down_pair = shift(jnp.concatenate([block[7], block[5]], axis=0), -1)
    near_up, via_up = up_pair[:rows], up_pair[rows:]
    near_down, via_down = down_pair[:rows], down_pair[rows:]
    far_up = shift(block[4][:top], 2)
    far_down = shift(block[4][top:], -2)
    zeros = jnp.zeros((rows - top, cols), jnp.float32)
    agg_up = block[2].astype(jnp.float32) + via_up + jnp.concatenate([far_up, zeros], axis=0)
    agg_down = block[6].astype(jnp.float32) + via_down + jnp.concatenate([zeros, far_down], axis=0)
    acc = acc + near_up + near_down
    acc = acc + shift(agg_up.astype(jnp.bfloat16), 2)
    acc = acc + shift(agg_down.astype(jnp.bfloat16), -2)
    return acc


def dispatch_rows(placements, sources, n_exp, capacity, n_core):
    core = lax.axis_index("core")
    share = sources[0].shape[1]
    sent = jnp.concatenate(
        [
            jnp.dot(placed_rows, source, preferred_element_type=jnp.float32).astype(jnp.bfloat16)
            for placed_rows, source in zip(placements, sources)
        ],
        axis=1,
    )
    got = lax.all_to_all(
        sent.reshape(n_exp, capacity, sent.shape[1]), "exp", split_axis=0, concat_axis=0, tiled=True
    ).reshape(n_exp * capacity, sent.shape[1])
    other = lax.ppermute(got, "core", [(j, (j + 1) % n_core) for j in range(n_core)])
    pair = jnp.stack([got, other])
    first, second = pick(pair, core, 0), pick(pair, 1 - core, 0)
    return [
        jnp.concatenate([first[:, i * share : (i + 1) * share], second[:, i * share : (i + 1) * share]], axis=1)
        for i in range(len(sources))
    ]


def local(tokens, expert_ids, gate_values, grad_out, w_up, w_down):
    n_z = lax.axis_size("z")
    n_core = lax.axis_size("core")
    n_rep = n_z * n_core
    n_exp = lax.axis_size("exp")
    tok_count, width = tokens.shape
    top_k = expert_ids.shape[1]
    pair_count = tok_count * top_k
    capacity = max(2, min(tok_count, 2 * tok_count * top_k // n_exp))
    cols = width // n_rep
    up_weight = w_up[0]
    down_weight = w_down[0]
    ff_local = up_weight.shape[1]
    zi = lax.axis_index("z")
    core = lax.axis_index("core")
    down_blocks = jnp.roll(down_weight.reshape(ff_local, n_z, n_core, cols), (-zi, -core), (1, 2))
    down_perm = down_blocks.transpose(0, 2, 1, 3).reshape(ff_local, width)
    up_blocks = jnp.roll(up_weight.reshape(n_z, n_core, cols, ff_local), (-zi, -core), (0, 1))
    up_perm = up_blocks.transpose(1, 0, 2, 3).reshape(width, ff_local)
    share = width // n_core
    tok_half = lax.dynamic_slice_in_dim(tokens, core * share, share, 1)
    grad_half = lax.dynamic_slice_in_dim(grad_out, core * share, share, 1)
    grad_rows = (gate_values[:, :, None] * grad_half[:, None, :].astype(jnp.float32)).astype(
        jnp.bfloat16
    )
    grad_rows = grad_rows.reshape(pair_count, share)
    placed, _ = plan_slots(expert_ids, n_exp, capacity)
    summed = placed.reshape(n_exp * capacity, tok_count, top_k).sum(axis=2)
    rows_in, rows_grad = dispatch_rows((summed, placed), (tok_half, grad_rows), n_exp, capacity, n_core)
    out_part, dx_part, grad_up_e, grad_down_e = expert_math(
        rows_in, rows_grad, up_weight, down_weight, up_perm, down_perm
    )
    acc = reduce_over_rep(
        (out_part.astype(jnp.bfloat16), dx_part.astype(jnp.bfloat16)), n_z, n_core, cols
    )
    slots = n_exp * capacity
    both = jnp.concatenate([acc[:slots], acc[slots:]], axis=1).astype(jnp.bfloat16)
    back_both = lax.all_to_all(
        both.reshape(n_exp, capacity, 2 * cols), "exp", split_axis=0, concat_axis=0, tiled=True
    ).reshape(n_exp * capacity, 2 * cols)
    back_out = back_both[:, :cols]
    back_dx = back_both[:, cols:]
    pair_out = jnp.einsum(
        "st,sd->td",
        placed,
        back_out,
        preferred_element_type=jnp.float32,
    )
    pair_dx = jnp.einsum(
        "st,sd->td",
        placed,
        back_dx,
        preferred_element_type=jnp.float32,
    )
    mixed = jnp.sum(gate_values[:, :, None] * pair_out.reshape(tok_count, top_k, cols), axis=1)
    grad_tokens = jnp.sum(pair_dx.reshape(tok_count, top_k, cols), axis=1)
    return (
        mixed.astype(jnp.bfloat16),
        grad_tokens.astype(jnp.bfloat16),
        grad_up_e.astype(jnp.bfloat16)[None],
        grad_down_e.astype(jnp.bfloat16)[None],
    )


def solution(mesh):
    n_rep, n_exp = mesh.devices.shape
    n_core = 2
    mesh3 = Mesh(mesh.devices.reshape(n_rep // n_core, n_core, n_exp), ("z", "core", "exp"))
    rep = ("z", "core")
    return jax.shard_map(
        local,
        mesh=mesh3,
        in_specs=(
            P("exp", None),
            P("exp", None),
            P("exp", None),
            P("exp", None),
            P("exp", None, rep),
            P("exp", rep, None),
        ),
        out_specs=(P("exp", rep), P("exp", rep), P("exp", None, rep), P("exp", rep, None)),
        check_vma=False,
    )
```

```python
import jax
import jax.numpy as jnp
from jax import lax
from jax.sharding import Mesh, PartitionSpec as P


def plan_slots(routed, experts, capacity):
    flat_ids = routed.reshape(-1)
    onehot = (flat_ids[:, None] == jnp.arange(experts, dtype=jnp.int32)[None, :]).astype(jnp.int32)
    before = jnp.cumsum(onehot, axis=0) - onehot
    position = jnp.sum(before * onehot, axis=1)
    counts = jnp.sum(onehot, axis=0)
    slotting_labels = flat_ids * capacity + position
    placed = (
        slotting_labels[None, :] == jnp.arange(experts * capacity, dtype=jnp.int32)[:, None]
    ).astype(jnp.bfloat16)
    return (placed, counts)


def expert_math(rows_in, rows_grad, up_weight, down_weight, up_perm, down_perm):
    preact = jnp.dot(rows_in, up_weight, preferred_element_type=jnp.float32)
    sigmoid_val = jax.nn.sigmoid(preact)
    hidden_units = (preact * sigmoid_val).astype(jnp.bfloat16)
    out_part = jnp.dot(hidden_units, down_perm, preferred_element_type=jnp.float32)
    grad_hidden = lax.dot_general(
        rows_grad, down_weight, (((1,), (1,)), ((), ())), preferred_element_type=jnp.float32
    )
    slope = sigmoid_val * (1.0 + preact * (1.0 - sigmoid_val))
    gradient_before_activation = (grad_hidden * slope).astype(jnp.bfloat16)
    dx_part = lax.dot_general(
        gradient_before_activation,
        up_perm,
        (((1,), (1,)), ((), ())),
        preferred_element_type=jnp.float32,
    )
    grad_down_e = lax.dot_general(
        hidden_units, rows_grad, (((0,), (0,)), ((), ())), preferred_element_type=jnp.float32
    )
    grad_up_e = lax.dot_general(
        rows_in,
        gradient_before_activation,
        (((0,), (0,)), ((), ())),
        preferred_element_type=jnp.float32,
    )
    return (out_part, dx_part, grad_up_e, grad_down_e)


def pick(stacked, index, axis):
    return lax.dynamic_index_in_dim(stacked, index, axis=axis, keepdims=False)


def reduce_over_rep(parts, n_z, n_core, cols):
    share = n_z * cols
    got = lax.ppermute(
        jnp.concatenate([p[:, share:] for p in parts], axis=0),
        "core",
        [(j, (j + 1) % n_core) for j in range(n_core)],
    )
    own = jnp.concatenate([p[:, :share] for p in parts], axis=0)
    pair_sum = (own.astype(jnp.float32) + got.astype(jnp.float32)).astype(jnp.bfloat16)
    block = [pair_sum[:, k * cols : (k + 1) * cols] for k in range(n_z)]
    acc = block[0].astype(jnp.float32)
    if n_z != 8:
        for k in range(1, n_z):
            moved = lax.ppermute(block[k], "z", [(j, (j + k) % n_z) for j in range(n_z)])
            acc = acc + moved.astype(jnp.float32)
        return acc

    def shift(x, k):
        return lax.ppermute(x, "z", [(j, (j + k) % n_z) for j in range(n_z)]).astype(jnp.float32)

    rows = pair_sum.shape[0]
    top = rows // 2
    near_up = shift(block[1], 1)
    near_down = shift(block[7], -1)
    via_up = shift(block[3], 1)
    via_down = shift(block[5], -1)
    far_up = shift(block[4][:top], 2)
    far_down = shift(block[4][top:], -2)
    zeros = jnp.zeros((rows - top, cols), jnp.float32)
    agg_up = block[2].astype(jnp.float32) + via_up + jnp.concatenate([far_up, zeros], axis=0)
    agg_down = block[6].astype(jnp.float32) + via_down + jnp.concatenate([zeros, far_down], axis=0)
    acc = acc + near_up + near_down
    acc = acc + shift(agg_up.astype(jnp.bfloat16), 2)
    acc = acc + shift(agg_down.astype(jnp.bfloat16), -2)
    return acc


def dispatch_rows(placements, sources, n_exp, capacity, n_core):
    core = lax.axis_index("core")
    share = sources[0].shape[1]
    sent = jnp.concatenate(
        [
            jnp.dot(placed_rows, source, preferred_element_type=jnp.float32).astype(jnp.bfloat16)
            for placed_rows, source in zip(placements, sources)
        ],
        axis=1,
    )
    got = lax.all_to_all(
        sent.reshape(n_exp, capacity, sent.shape[1]), "exp", split_axis=0, concat_axis=0, tiled=True
    ).reshape(n_exp * capacity, sent.shape[1])
    swap = [(j, (j + 1) % n_core) for j in range(n_core)]
    rows = []
    for i in range(len(sources)):
        mine = got[:, i * share : (i + 1) * share]
        other = lax.ppermute(mine, "core", swap)
        pair = jnp.stack([mine, other])
        rows.append(jnp.concatenate([pick(pair, core, 0), pick(pair, 1 - core, 0)], axis=1))
    return rows


def local(tokens, expert_ids, gate_values, grad_out, w_up, w_down):
    n_z = lax.axis_size("z")
    n_core = lax.axis_size("core")
    n_rep = n_z * n_core
    n_exp = lax.axis_size("exp")
    tok_count, width = tokens.shape
    top_k = expert_ids.shape[1]
    pair_count = tok_count * top_k
    capacity = max(2, min(tok_count, 2 * tok_count * top_k // n_exp))
    cols = width // n_rep
    up_weight = w_up[0]
    down_weight = w_down[0]
    ff_local = up_weight.shape[1]
    zi = lax.axis_index("z")
    core = lax.axis_index("core")
    down_blocks = jnp.roll(down_weight.reshape(ff_local, n_z, n_core, cols), (-zi, -core), (1, 2))
    down_perm = down_blocks.transpose(0, 2, 1, 3).reshape(ff_local, width)
    up_blocks = jnp.roll(up_weight.reshape(n_z, n_core, cols, ff_local), (-zi, -core), (0, 1))
    up_perm = up_blocks.transpose(1, 0, 2, 3).reshape(width, ff_local)
    share = width // n_core
    tok_half = lax.dynamic_slice_in_dim(tokens, core * share, share, 1)
    grad_half = lax.dynamic_slice_in_dim(grad_out, core * share, share, 1)
    grad_rows = (gate_values[:, :, None] * grad_half[:, None, :].astype(jnp.float32)).astype(
        jnp.bfloat16
    )
    grad_rows = grad_rows.reshape(pair_count, share)
    placed, _ = plan_slots(expert_ids, n_exp, capacity)
    summed = placed.reshape(n_exp * capacity, tok_count, top_k).sum(axis=2)
    rows_in, rows_grad = dispatch_rows((summed, placed), (tok_half, grad_rows), n_exp, capacity, n_core)
    out_part, dx_part, grad_up_e, grad_down_e = expert_math(
        rows_in, rows_grad, up_weight, down_weight, up_perm, down_perm
    )
    acc = reduce_over_rep(
        (out_part.astype(jnp.bfloat16), dx_part.astype(jnp.bfloat16)), n_z, n_core, cols
    )
    slots = n_exp * capacity
    both = jnp.concatenate([acc[:slots], acc[slots:]], axis=1).astype(jnp.bfloat16)
    back_both = lax.all_to_all(
        both.reshape(n_exp, capacity, 2 * cols), "exp", split_axis=0, concat_axis=0, tiled=True
    ).reshape(n_exp * capacity, 2 * cols)
    back_out = back_both[:, :cols]
    back_dx = back_both[:, cols:]
    pair_out = jnp.einsum(
        "st,sd->td",
        placed,
        back_out,
        preferred_element_type=jnp.float32,
    )
    pair_dx = jnp.einsum(
        "st,sd->td",
        placed,
        back_dx,
        preferred_element_type=jnp.float32,
    )
    mixed = jnp.sum(gate_values[:, :, None] * pair_out.reshape(tok_count, top_k, cols), axis=1)
    grad_tokens = jnp.sum(pair_dx.reshape(tok_count, top_k, cols), axis=1)
    return (
        mixed.astype(jnp.bfloat16),
        grad_tokens.astype(jnp.bfloat16),
        grad_up_e.astype(jnp.bfloat16)[None],
        grad_down_e.astype(jnp.bfloat16)[None],
    )


def solution(mesh):
    n_rep, n_exp = mesh.devices.shape
    n_core = 2
    mesh3 = Mesh(mesh.devices.reshape(n_rep // n_core, n_core, n_exp), ("z", "core", "exp"))
    rep = ("z", "core")
    return jax.shard_map(
        local,
        mesh=mesh3,
        in_specs=(
            P("exp", None),
            P("exp", None),
            P("exp", None),
            P("exp", None),
            P("exp", None, rep),
            P("exp", rep, None),
        ),
        out_specs=(P("exp", rep), P("exp", rep), P("exp", None, rep), P("exp", rep, None)),
        check_vma=False,
    )
```

```python
import jax
import jax.numpy as jnp
from jax import lax
from jax.sharding import Mesh, PartitionSpec as P


def plan_slots(routed, experts, capacity):
    flat_ids = routed.reshape(-1)
    onehot = (flat_ids[:, None] == jnp.arange(experts, dtype=jnp.int32)[None, :]).astype(jnp.int32)
    before = jnp.cumsum(onehot, axis=0) - onehot
    position = jnp.sum(before * onehot, axis=1)
    counts = jnp.sum(onehot, axis=0)
    slotting_labels = flat_ids * capacity + position
    placed = (
        slotting_labels[None, :] == jnp.arange(experts * capacity, dtype=jnp.int32)[:, None]
    ).astype(jnp.bfloat16)
    return (placed, counts)


def expert_math(rows_in, rows_grad, up_weight, down_weight, up_perm, down_perm):
    preact = jnp.dot(rows_in, up_weight, preferred_element_type=jnp.float32)
    sigmoid_val = jax.nn.sigmoid(preact)
    hidden_units = (preact * sigmoid_val).astype(jnp.bfloat16)
    out_part = jnp.dot(hidden_units, down_perm, preferred_element_type=jnp.float32)
    grad_hidden = lax.dot_general(
        rows_grad, down_weight, (((1,), (1,)), ((), ())), preferred_element_type=jnp.float32
    )
    slope = sigmoid_val * (1.0 + preact * (1.0 - sigmoid_val))
    gradient_before_activation = (grad_hidden * slope).astype(jnp.bfloat16)
    dx_part = lax.dot_general(
        gradient_before_activation,
        up_perm,
        (((1,), (1,)), ((), ())),
        preferred_element_type=jnp.float32,
    )
    grad_down_e = lax.dot_general(
        hidden_units, rows_grad, (((0,), (0,)), ((), ())), preferred_element_type=jnp.float32
    )
    grad_up_e = lax.dot_general(
        rows_in,
        gradient_before_activation,
        (((0,), (0,)), ((), ())),
        preferred_element_type=jnp.float32,
    )
    return (out_part, dx_part, grad_up_e, grad_down_e)


def pick(stacked, index, axis):
    return lax.dynamic_index_in_dim(stacked, index, axis=axis, keepdims=False)


def reduce_round_a(part, n_z, n_core, cols):
    share = n_z * cols
    got = lax.ppermute(part[:, share:], "core", [(j, (j + 1) % n_core) for j in range(n_core)])
    pair_sum = (part[:, :share].astype(jnp.float32) + got.astype(jnp.float32)).astype(jnp.bfloat16)
    block = [pair_sum[:, k * cols : (k + 1) * cols] for k in range(n_z)]
    acc = block[0].astype(jnp.float32)
    if n_z != 8:
        for k in range(1, n_z):
            acc = acc + shift_z(block[k], k, n_z)
        return acc, None, None
    rows = pair_sum.shape[0]
    top = rows // 2
    acc = acc + shift_z(block[1], 1, n_z) + shift_z(block[7], -1, n_z)
    zeros = jnp.zeros((rows - top, cols), jnp.float32)
    far_up = jnp.concatenate([shift_z(block[4][:top], 2, n_z), zeros], axis=0)
    far_down = jnp.concatenate([zeros, shift_z(block[4][top:], -2, n_z)], axis=0)
    agg_up = block[2].astype(jnp.float32) + shift_z(block[3], 1, n_z) + far_up
    agg_down = block[6].astype(jnp.float32) + shift_z(block[5], -1, n_z) + far_down
    return acc, agg_up, agg_down


def shift_z(x, k, n_z):
    return lax.ppermute(x, "z", [(j, (j + k) % n_z) for j in range(n_z)]).astype(jnp.float32)


def reduce_round_b(stages, n_z):
    accs = jnp.concatenate([s[0] for s in stages], axis=0)
    if stages[0][1] is None:
        return accs
    agg_up = jnp.concatenate([s[1] for s in stages], axis=0).astype(jnp.bfloat16)
    agg_down = jnp.concatenate([s[2] for s in stages], axis=0).astype(jnp.bfloat16)
    return accs + shift_z(agg_up, 2, n_z) + shift_z(agg_down, -2, n_z)


def dispatch_rows(placements, sources, n_exp, capacity, n_core):
    core = lax.axis_index("core")
    share = sources[0].shape[1]
    sent = jnp.concatenate(
        [
            jnp.dot(placed_rows, source, preferred_element_type=jnp.float32).astype(jnp.bfloat16)
            for placed_rows, source in zip(placements, sources)
        ],
        axis=1,
    )
    got = lax.all_to_all(
        sent.reshape(n_exp, capacity, sent.shape[1]), "exp", split_axis=0, concat_axis=0, tiled=True
    ).reshape(n_exp * capacity, sent.shape[1])
    other = lax.ppermute(got, "core", [(j, (j + 1) % n_core) for j in range(n_core)])
    pair = jnp.stack([got, other])
    first, second = pick(pair, core, 0), pick(pair, 1 - core, 0)
    return [
        jnp.concatenate([first[:, i * share : (i + 1) * share], second[:, i * share : (i + 1) * share]], axis=1)
        for i in range(len(sources))
    ]


def local(tokens, expert_ids, gate_values, grad_out, w_up, w_down):
    n_z = lax.axis_size("z")
    n_core = lax.axis_size("core")
    n_rep = n_z * n_core
    n_exp = lax.axis_size("exp")
    tok_count, width = tokens.shape
    top_k = expert_ids.shape[1]
    pair_count = tok_count * top_k
    capacity = max(2, min(tok_count, 2 * tok_count * top_k // n_exp))
    cols = width // n_rep
    up_weight = w_up[0]
    down_weight = w_down[0]
    ff_local = up_weight.shape[1]
    zi = lax.axis_index("z")
    core = lax.axis_index("core")
    down_blocks = jnp.roll(down_weight.reshape(ff_local, n_z, n_core, cols), (-zi, -core), (1, 2))
    down_perm = down_blocks.transpose(0, 2, 1, 3).reshape(ff_local, width)
    up_blocks = jnp.roll(up_weight.reshape(n_z, n_core, cols, ff_local), (-zi, -core), (0, 1))
    up_perm = up_blocks.transpose(1, 0, 2, 3).reshape(width, ff_local)
    share = width // n_core
    tok_half = lax.dynamic_slice_in_dim(tokens, core * share, share, 1)
    grad_half = lax.dynamic_slice_in_dim(grad_out, core * share, share, 1)
    grad_rows = (gate_values[:, :, None] * grad_half[:, None, :].astype(jnp.float32)).astype(
        jnp.bfloat16
    )
    grad_rows = grad_rows.reshape(pair_count, share)
    placed, _ = plan_slots(expert_ids, n_exp, capacity)
    summed = placed.reshape(n_exp * capacity, tok_count, top_k).sum(axis=2)
    rows_in, rows_grad = dispatch_rows((summed, placed), (tok_half, grad_rows), n_exp, capacity, n_core)
    out_part, dx_part, grad_up_e, grad_down_e = expert_math(
        rows_in, rows_grad, up_weight, down_weight, up_perm, down_perm
    )
    stages = [reduce_round_a(p.astype(jnp.bfloat16), n_z, n_core, cols) for p in (out_part, dx_part)]
    acc = reduce_round_b(stages, n_z)
    slots = n_exp * capacity
    both = jnp.concatenate([acc[:slots], acc[slots:]], axis=1).astype(jnp.bfloat16)
    back_both = lax.all_to_all(
        both.reshape(n_exp, capacity, 2 * cols), "exp", split_axis=0, concat_axis=0, tiled=True
    ).reshape(n_exp * capacity, 2 * cols)
    back_out = back_both[:, :cols]
    back_dx = back_both[:, cols:]
    pair_out = jnp.einsum(
        "st,sd->td",
        placed,
        back_out,
        preferred_element_type=jnp.float32,
    )
    pair_dx = jnp.einsum(
        "st,sd->td",
        placed,
        back_dx,
        preferred_element_type=jnp.float32,
    )
    mixed = jnp.sum(gate_values[:, :, None] * pair_out.reshape(tok_count, top_k, cols), axis=1)
    grad_tokens = jnp.sum(pair_dx.reshape(tok_count, top_k, cols), axis=1)
    return (
        mixed.astype(jnp.bfloat16),
        grad_tokens.astype(jnp.bfloat16),
        grad_up_e.astype(jnp.bfloat16)[None],
        grad_down_e.astype(jnp.bfloat16)[None],
    )


def solution(mesh):
    n_rep, n_exp = mesh.devices.shape
    n_core = 2
    mesh3 = Mesh(mesh.devices.reshape(n_rep // n_core, n_core, n_exp), ("z", "core", "exp"))
    rep = ("z", "core")
    return jax.shard_map(
        local,
        mesh=mesh3,
        in_specs=(
            P("exp", None),
            P("exp", None),
            P("exp", None),
            P("exp", None),
            P("exp", None, rep),
            P("exp", rep, None),
        ),
        out_specs=(P("exp", rep), P("exp", rep), P("exp", None, rep), P("exp", rep, None)),
        check_vma=False,
    )
```

```python
import jax
import jax.numpy as jnp
from jax import lax
from jax.sharding import Mesh, PartitionSpec as P


def plan_slots(routed, experts, capacity):
    flat_ids = routed.reshape(-1)
    onehot = (flat_ids[:, None] == jnp.arange(experts, dtype=jnp.int32)[None, :]).astype(jnp.int32)
    before = jnp.cumsum(onehot, axis=0) - onehot
    position = jnp.sum(before * onehot, axis=1)
    counts = jnp.sum(onehot, axis=0)
    slotting_labels = flat_ids * capacity + position
    placed = (
        slotting_labels[None, :] == jnp.arange(experts * capacity, dtype=jnp.int32)[:, None]
    ).astype(jnp.bfloat16)
    return (placed, counts)


def expert_math(rows_in, rows_grad, up_weight, down_weight, up_perm, down_perm):
    preact = jnp.dot(rows_in, up_weight, preferred_element_type=jnp.float32)
    sigmoid_val = jax.nn.sigmoid(preact)
    hidden_units = (preact * sigmoid_val).astype(jnp.bfloat16)
    out_part = jnp.dot(hidden_units, down_perm, preferred_element_type=jnp.float32)
    grad_hidden = lax.dot_general(
        rows_grad, down_weight, (((1,), (1,)), ((), ())), preferred_element_type=jnp.float32
    )
    slope = sigmoid_val * (1.0 + preact * (1.0 - sigmoid_val))
    gradient_before_activation = (grad_hidden * slope).astype(jnp.bfloat16)
    dx_part = lax.dot_general(
        gradient_before_activation,
        up_perm,
        (((1,), (1,)), ((), ())),
        preferred_element_type=jnp.float32,
    )
    grad_down_e = lax.dot_general(
        hidden_units, rows_grad, (((0,), (0,)), ((), ())), preferred_element_type=jnp.float32
    )
    grad_up_e = lax.dot_general(
        rows_in,
        gradient_before_activation,
        (((0,), (0,)), ((), ())),
        preferred_element_type=jnp.float32,
    )
    return (out_part, dx_part, grad_up_e, grad_down_e)


def pick(stacked, index, axis):
    return lax.dynamic_index_in_dim(stacked, index, axis=axis, keepdims=False)


def block_order(n_z):
    return (1, 7, 3, 5, 4, 2, 6, 0) if n_z == 8 else tuple(range(n_z))


def reduce_over_rep(parts, n_z, n_core, cols):
    share = n_z * cols
    order = block_order(n_z)
    lead = 5 if n_z == 8 else n_z
    swap = [(j, (j + 1) % n_core) for j in range(n_core)]
    sums = []
    for lo, hi in ((0, lead), (lead, n_z)):
        if lo == hi:
            continue
        got = lax.ppermute(
            jnp.concatenate([p[:, share + lo * cols : share + hi * cols] for p in parts], axis=0),
            "core",
            swap,
        )
        own = jnp.concatenate([p[:, lo * cols : hi * cols] for p in parts], axis=0)
        sums.append((own.astype(jnp.float32) + got.astype(jnp.float32)).astype(jnp.bfloat16))
    block = {}
    for i, offset in enumerate(order):
        src_sum, at = (sums[0], i) if i < lead else (sums[1], i - lead)
        block[offset] = src_sum[:, at * cols : (at + 1) * cols]
    acc = block[0].astype(jnp.float32)
    if n_z != 8:
        for k in range(1, n_z):
            moved = lax.ppermute(block[k], "z", [(j, (j + k) % n_z) for j in range(n_z)])
            acc = acc + moved.astype(jnp.float32)
        return acc

    def shift(x, k):
        return lax.ppermute(x, "z", [(j, (j + k) % n_z) for j in range(n_z)]).astype(jnp.float32)

    rows = acc.shape[0]
    top = rows // 2
    near_up = shift(block[1], 1)
    near_down = shift(block[7], -1)
    via_up = shift(block[3], 1)
    via_down = shift(block[5], -1)
    far_up = shift(block[4][:top], 2)
    far_down = shift(block[4][top:], -2)
    zeros = jnp.zeros((rows - top, cols), jnp.float32)
    agg_up = block[2].astype(jnp.float32) + via_up + jnp.concatenate([far_up, zeros], axis=0)
    agg_down = block[6].astype(jnp.float32) + via_down + jnp.concatenate([zeros, far_down], axis=0)
    acc = acc + near_up + near_down
    acc = acc + shift(agg_up.astype(jnp.bfloat16), 2)
    acc = acc + shift(agg_down.astype(jnp.bfloat16), -2)
    return acc


def dispatch_rows(placements, sources, n_exp, capacity, n_core):
    core = lax.axis_index("core")
    share = sources[0].shape[1]
    sent = jnp.concatenate(
        [
            jnp.dot(placed_rows, source, preferred_element_type=jnp.float32).astype(jnp.bfloat16)
            for placed_rows, source in zip(placements, sources)
        ],
        axis=1,
    )
    got = lax.all_to_all(
        sent.reshape(n_exp, capacity, sent.shape[1]), "exp", split_axis=0, concat_axis=0, tiled=True
    ).reshape(n_exp * capacity, sent.shape[1])
    other = lax.ppermute(got, "core", [(j, (j + 1) % n_core) for j in range(n_core)])
    pair = jnp.stack([got, other])
    first, second = pick(pair, core, 0), pick(pair, 1 - core, 0)
    return [
        jnp.concatenate([first[:, i * share : (i + 1) * share], second[:, i * share : (i + 1) * share]], axis=1)
        for i in range(len(sources))
    ]


def local(tokens, expert_ids, gate_values, grad_out, w_up, w_down):
    n_z = lax.axis_size("z")
    n_core = lax.axis_size("core")
    n_rep = n_z * n_core
    n_exp = lax.axis_size("exp")
    tok_count, width = tokens.shape
    top_k = expert_ids.shape[1]
    pair_count = tok_count * top_k
    capacity = max(2, min(tok_count, 2 * tok_count * top_k // n_exp))
    cols = width // n_rep
    up_weight = w_up[0]
    down_weight = w_down[0]
    ff_local = up_weight.shape[1]
    zi = lax.axis_index("z")
    core = lax.axis_index("core")
    order = jnp.array(block_order(n_z), jnp.int32)
    down_blocks = jnp.roll(down_weight.reshape(ff_local, n_z, n_core, cols), (-zi, -core), (1, 2))
    down_blocks = jnp.take(down_blocks, order, axis=1)
    down_perm = down_blocks.transpose(0, 2, 1, 3).reshape(ff_local, width)
    up_blocks = jnp.roll(up_weight.reshape(n_z, n_core, cols, ff_local), (-zi, -core), (0, 1))
    up_blocks = jnp.take(up_blocks, order, axis=0)
    up_perm = up_blocks.transpose(1, 0, 2, 3).reshape(width, ff_local)
    share = width // n_core
    tok_half = lax.dynamic_slice_in_dim(tokens, core * share, share, 1)
    grad_half = lax.dynamic_slice_in_dim(grad_out, core * share, share, 1)
    grad_rows = (gate_values[:, :, None] * grad_half[:, None, :].astype(jnp.float32)).astype(
        jnp.bfloat16
    )
    grad_rows = grad_rows.reshape(pair_count, share)
    placed, _ = plan_slots(expert_ids, n_exp, capacity)
    summed = placed.reshape(n_exp * capacity, tok_count, top_k).sum(axis=2)
    rows_in, rows_grad = dispatch_rows((summed, placed), (tok_half, grad_rows), n_exp, capacity, n_core)
    out_part, dx_part, grad_up_e, grad_down_e = expert_math(
        rows_in, rows_grad, up_weight, down_weight, up_perm, down_perm
    )
    acc = reduce_over_rep(
        (out_part.astype(jnp.bfloat16), dx_part.astype(jnp.bfloat16)), n_z, n_core, cols
    )
    slots = n_exp * capacity
    both = jnp.concatenate([acc[:slots], acc[slots:]], axis=1).astype(jnp.bfloat16)
    back_both = lax.all_to_all(
        both.reshape(n_exp, capacity, 2 * cols), "exp", split_axis=0, concat_axis=0, tiled=True
    ).reshape(n_exp * capacity, 2 * cols)
    back_out = back_both[:, :cols]
    back_dx = back_both[:, cols:]
    pair_out = jnp.einsum(
        "st,sd->td",
        placed,
        back_out,
        preferred_element_type=jnp.float32,
    )
    pair_dx = jnp.einsum(
        "st,sd->td",
        placed,
        back_dx,
        preferred_element_type=jnp.float32,
    )
    mixed = jnp.sum(gate_values[:, :, None] * pair_out.reshape(tok_count, top_k, cols), axis=1)
    grad_tokens = jnp.sum(pair_dx.reshape(tok_count, top_k, cols), axis=1)
    return (
        mixed.astype(jnp.bfloat16),
        grad_tokens.astype(jnp.bfloat16),
        grad_up_e.astype(jnp.bfloat16)[None],
        grad_down_e.astype(jnp.bfloat16)[None],
    )


def solution(mesh):
    n_rep, n_exp = mesh.devices.shape
    n_core = 2
    mesh3 = Mesh(mesh.devices.reshape(n_rep // n_core, n_core, n_exp), ("z", "core", "exp"))
    rep = ("z", "core")
    return jax.shard_map(
        local,
        mesh=mesh3,
        in_specs=(
            P("exp", None),
            P("exp", None),
            P("exp", None),
            P("exp", None),
            P("exp", None, rep),
            P("exp", rep, None),
        ),
        out_specs=(P("exp", rep), P("exp", rep), P("exp", None, rep), P("exp", rep, None)),
        check_vma=False,
    )
```

```python
import jax
import jax.numpy as jnp
from jax import lax
from jax.sharding import Mesh, PartitionSpec as P


def plan_slots(routed, experts, capacity):
    flat_ids = routed.reshape(-1)
    onehot = (flat_ids[:, None] == jnp.arange(experts, dtype=jnp.int32)[None, :]).astype(jnp.int32)
    before = jnp.cumsum(onehot, axis=0) - onehot
    position = jnp.sum(before * onehot, axis=1)
    counts = jnp.sum(onehot, axis=0)
    slotting_labels = flat_ids * capacity + position
    placed = (
        slotting_labels[None, :] == jnp.arange(experts * capacity, dtype=jnp.int32)[:, None]
    ).astype(jnp.bfloat16)
    return (placed, counts)


def expert_math(rows_in, rows_grad, up_weight, down_weight, up_perm, down_perm):
    preact = jnp.dot(rows_in, up_weight, preferred_element_type=jnp.float32)
    sigmoid_val = jax.nn.sigmoid(preact)
    hidden_units = (preact * sigmoid_val).astype(jnp.bfloat16)
    out_part = jnp.dot(hidden_units, down_perm, preferred_element_type=jnp.float32)
    grad_hidden = lax.dot_general(
        rows_grad, down_weight, (((1,), (1,)), ((), ())), preferred_element_type=jnp.float32
    )
    slope = sigmoid_val * (1.0 + preact * (1.0 - sigmoid_val))
    gradient_before_activation = (grad_hidden * slope).astype(jnp.bfloat16)
    dx_part = lax.dot_general(
        gradient_before_activation,
        up_perm,
        (((1,), (1,)), ((), ())),
        preferred_element_type=jnp.float32,
    )
    grad_down_e = lax.dot_general(
        hidden_units, rows_grad, (((0,), (0,)), ((), ())), preferred_element_type=jnp.float32
    )
    grad_up_e = lax.dot_general(
        rows_in,
        gradient_before_activation,
        (((0,), (0,)), ((), ())),
        preferred_element_type=jnp.float32,
    )
    return (out_part, dx_part, grad_up_e, grad_down_e)


def pick(stacked, index, axis):
    return lax.dynamic_index_in_dim(stacked, index, axis=axis, keepdims=False)


def reduce_over_rep(parts, n_z, n_core, cols):
    share = n_z * cols
    got = lax.ppermute(
        jnp.concatenate([p[:, share:] for p in parts], axis=0),
        "core",
        [(j, (j + 1) % n_core) for j in range(n_core)],
    )
    own = jnp.concatenate([p[:, :share] for p in parts], axis=0)
    pair_sum = (own.astype(jnp.float32) + got.astype(jnp.float32)).astype(jnp.bfloat16)
    block = [pair_sum[:, k * cols : (k + 1) * cols] for k in range(n_z)]
    acc = block[0].astype(jnp.float32)
    if n_z != 8:
        for k in range(1, n_z):
            moved = lax.ppermute(block[k], "z", [(j, (j + k) % n_z) for j in range(n_z)])
            acc = acc + moved.astype(jnp.float32)
        return acc

    def shift(x, k):
        return lax.ppermute(x, "z", [(j, (j + k) % n_z) for j in range(n_z)]).astype(jnp.float32)

    rows = pair_sum.shape[0]
    top = rows // 2
    near_up = shift(block[1], 1)
    near_down = shift(block[7], -1)
    via_up = shift(block[3], 1)
    via_down = shift(block[5], -1)
    far_up = shift(block[4][:top], 2)
    far_down = shift(block[4][top:], -2)
    zeros = jnp.zeros((rows - top, cols), jnp.float32)
    agg_up = block[2].astype(jnp.float32) + via_up + jnp.concatenate([far_up, zeros], axis=0)
    agg_down = block[6].astype(jnp.float32) + via_down + jnp.concatenate([zeros, far_down], axis=0)
    acc = acc + near_up + near_down
    acc = acc + shift(agg_up.astype(jnp.bfloat16), 2)
    acc = acc + shift(agg_down.astype(jnp.bfloat16), -2)
    return acc


def dispatch_rows(placements, sources, n_exp, capacity, n_core):
    core = lax.axis_index("core")
    share = sources[0].shape[1]
    sent = jnp.concatenate(
        [
            jnp.dot(placed_rows, source, preferred_element_type=jnp.float32).astype(jnp.bfloat16)
            for placed_rows, source in zip(placements, sources)
        ],
        axis=1,
    )
    got = lax.all_to_all(
        sent.reshape(n_exp, capacity, sent.shape[1]), "exp", split_axis=0, concat_axis=0, tiled=True
    ).reshape(n_exp * capacity, sent.shape[1])
    other = lax.ppermute(got, "core", [(j, (j + 1) % n_core) for j in range(n_core)])
    pair = jnp.stack([got, other])
    first, second = pick(pair, core, 0), pick(pair, 1 - core, 0)
    return [
        jnp.concatenate([first[:, i * share : (i + 1) * share], second[:, i * share : (i + 1) * share]], axis=1)
        for i in range(len(sources))
    ]


def local(tokens, expert_ids, gate_values, grad_out, w_up, w_down):
    n_z = lax.axis_size("z")
    n_core = lax.axis_size("core")
    n_rep = n_z * n_core
    n_exp = lax.axis_size("exp")
    tok_count, width = tokens.shape
    top_k = expert_ids.shape[1]
    pair_count = tok_count * top_k
    capacity = max(2, min(tok_count, 2 * tok_count * top_k // n_exp))
    cols = width // n_rep
    up_weight = w_up[0]
    down_weight = w_down[0]
    ff_local = up_weight.shape[1]
    zi = lax.axis_index("z")
    core = lax.axis_index("core")
    down_blocks = jnp.roll(down_weight.reshape(ff_local, n_z, n_core, cols), (-zi, -core), (1, 2))
    down_perm = down_blocks.transpose(0, 2, 1, 3).reshape(ff_local, width)
    up_blocks = jnp.roll(up_weight.reshape(n_z, n_core, cols, ff_local), (-zi, -core), (0, 1))
    up_perm = up_blocks.transpose(1, 0, 2, 3).reshape(width, ff_local)
    share = width // n_core
    tok_half = lax.dynamic_slice_in_dim(tokens, core * share, share, 1)
    grad_half = lax.dynamic_slice_in_dim(grad_out, core * share, share, 1)
    grad_rows = (gate_values[:, :, None] * grad_half[:, None, :].astype(jnp.float32)).astype(
        jnp.bfloat16
    )
    grad_rows = grad_rows.reshape(pair_count, share)
    placed, _ = plan_slots(expert_ids, n_exp, capacity)
    summed = placed.reshape(n_exp * capacity, tok_count, top_k).sum(axis=2)
    rows_in, rows_grad = dispatch_rows((summed, placed), (tok_half, grad_rows), n_exp, capacity, n_core)
    out_part, dx_part, grad_up_e, grad_down_e = expert_math(
        rows_in, rows_grad, up_weight, down_weight, up_perm, down_perm
    )
    acc = reduce_over_rep(
        (out_part.astype(jnp.bfloat16), dx_part.astype(jnp.bfloat16)), n_z, n_core, cols
    )
    slots = n_exp * capacity
    back_both = lax.all_to_all(
        acc.astype(jnp.bfloat16).reshape(2, n_exp, capacity, cols),
        "exp",
        split_axis=1,
        concat_axis=1,
        tiled=True,
    )
    back_out = back_both[0].reshape(slots, cols)
    back_dx = back_both[1].reshape(slots, cols)
    pair_out = jnp.einsum(
        "st,sd->td",
        placed,
        back_out,
        preferred_element_type=jnp.float32,
    )
    pair_dx = jnp.einsum(
        "st,sd->td",
        placed,
        back_dx,
        preferred_element_type=jnp.float32,
    )
    mixed = jnp.sum(gate_values[:, :, None] * pair_out.reshape(tok_count, top_k, cols), axis=1)
    grad_tokens = jnp.sum(pair_dx.reshape(tok_count, top_k, cols), axis=1)
    return (
        mixed.astype(jnp.bfloat16),
        grad_tokens.astype(jnp.bfloat16),
        grad_up_e.astype(jnp.bfloat16)[None],
        grad_down_e.astype(jnp.bfloat16)[None],
    )


def solution(mesh):
    n_rep, n_exp = mesh.devices.shape
    n_core = 2
    mesh3 = Mesh(mesh.devices.reshape(n_rep // n_core, n_core, n_exp), ("z", "core", "exp"))
    rep = ("z", "core")
    return jax.shard_map(
        local,
        mesh=mesh3,
        in_specs=(
            P("exp", None),
            P("exp", None),
            P("exp", None),
            P("exp", None),
            P("exp", None, rep),
            P("exp", rep, None),
        ),
        out_specs=(P("exp", rep), P("exp", rep), P("exp", None, rep), P("exp", rep, None)),
        check_vma=False,
    )
```

```python
import jax
import jax.numpy as jnp
from jax import lax
from jax.sharding import Mesh, PartitionSpec as P


def plan_slots(routed, experts, capacity):
    flat_ids = routed.reshape(-1)
    onehot = (flat_ids[:, None] == jnp.arange(experts, dtype=jnp.int32)[None, :]).astype(jnp.int32)
    before = jnp.cumsum(onehot, axis=0) - onehot
    position = jnp.sum(before * onehot, axis=1)
    counts = jnp.sum(onehot, axis=0)
    slotting_labels = flat_ids * capacity + position
    placed = (
        slotting_labels[None, :] == jnp.arange(experts * capacity, dtype=jnp.int32)[:, None]
    ).astype(jnp.bfloat16)
    return (placed, counts)


def expert_math(rows_in, rows_grad, up_weight, down_weight, up_perm, down_perm):
    preact = jnp.dot(rows_in, up_weight, preferred_element_type=jnp.float32)
    sigmoid_val = jax.nn.sigmoid(preact)
    hidden_units = (preact * sigmoid_val).astype(jnp.bfloat16)
    out_part = jnp.dot(hidden_units, down_perm, preferred_element_type=jnp.float32)
    grad_hidden = lax.dot_general(
        rows_grad, down_weight, (((1,), (1,)), ((), ())), preferred_element_type=jnp.float32
    )
    slope = sigmoid_val * (1.0 + preact * (1.0 - sigmoid_val))
    gradient_before_activation = (grad_hidden * slope).astype(jnp.bfloat16)
    dx_part = lax.dot_general(
        gradient_before_activation,
        up_perm,
        (((1,), (1,)), ((), ())),
        preferred_element_type=jnp.float32,
    )
    grad_down_e = lax.dot_general(
        hidden_units, rows_grad, (((0,), (0,)), ((), ())), preferred_element_type=jnp.float32
    )
    grad_up_e = lax.dot_general(
        rows_in,
        gradient_before_activation,
        (((0,), (0,)), ((), ())),
        preferred_element_type=jnp.float32,
    )
    return (out_part, dx_part, grad_up_e, grad_down_e)


def pick(stacked, index, axis):
    return lax.dynamic_index_in_dim(stacked, index, axis=axis, keepdims=False)


def reduce_over_rep(parts, n_z, n_core, cols):
    share = n_z * cols
    swap = [(j, (j + 1) % n_core) for j in range(n_core)]
    pair_sum = jnp.concatenate(
        [
            (
                p[:, :share].astype(jnp.float32)
                + lax.ppermute(p[:, share:], "core", swap).astype(jnp.float32)
            ).astype(jnp.bfloat16)
            for p in parts
        ],
        axis=0,
    )
    block = [pair_sum[:, k * cols : (k + 1) * cols] for k in range(n_z)]
    acc = block[0].astype(jnp.float32)
    if n_z != 8:
        for k in range(1, n_z):
            moved = lax.ppermute(block[k], "z", [(j, (j + k) % n_z) for j in range(n_z)])
            acc = acc + moved.astype(jnp.float32)
        return acc

    def shift(x, k):
        return lax.ppermute(x, "z", [(j, (j + k) % n_z) for j in range(n_z)]).astype(jnp.float32)

    rows = pair_sum.shape[0]
    top = rows // 2
    near_up = shift(block[1], 1)
    near_down = shift(block[7], -1)
    via_up = shift(block[3], 1)
    via_down = shift(block[5], -1)
    far_up = shift(block[4][:top], 2)
    far_down = shift(block[4][top:], -2)
    zeros = jnp.zeros((rows - top, cols), jnp.float32)
    agg_up = block[2].astype(jnp.float32) + via_up + jnp.concatenate([far_up, zeros], axis=0)
    agg_down = block[6].astype(jnp.float32) + via_down + jnp.concatenate([zeros, far_down], axis=0)
    acc = acc + near_up + near_down
    acc = acc + shift(agg_up.astype(jnp.bfloat16), 2)
    acc = acc + shift(agg_down.astype(jnp.bfloat16), -2)
    return acc


def dispatch_rows(placements, sources, n_exp, capacity, n_core):
    core = lax.axis_index("core")
    share = sources[0].shape[1]
    sent = jnp.concatenate(
        [
            jnp.dot(placed_rows, source, preferred_element_type=jnp.float32).astype(jnp.bfloat16)
            for placed_rows, source in zip(placements, sources)
        ],
        axis=1,
    )
    got = lax.all_to_all(
        sent.reshape(n_exp, capacity, sent.shape[1]), "exp", split_axis=0, concat_axis=0, tiled=True
    ).reshape(n_exp * capacity, sent.shape[1])
    other = lax.ppermute(got, "core", [(j, (j + 1) % n_core) for j in range(n_core)])
    pair = jnp.stack([got, other])
    first, second = pick(pair, core, 0), pick(pair, 1 - core, 0)
    return [
        jnp.concatenate([first[:, i * share : (i + 1) * share], second[:, i * share : (i + 1) * share]], axis=1)
        for i in range(len(sources))
    ]


def local(tokens, expert_ids, gate_values, grad_out, w_up, w_down):
    n_z = lax.axis_size("z")
    n_core = lax.axis_size("core")
    n_rep = n_z * n_core
    n_exp = lax.axis_size("exp")
    tok_count, width = tokens.shape
    top_k = expert_ids.shape[1]
    pair_count = tok_count * top_k
    capacity = max(2, min(tok_count, 2 * tok_count * top_k // n_exp))
    cols = width // n_rep
    up_weight = w_up[0]
    down_weight = w_down[0]
    ff_local = up_weight.shape[1]
    zi = lax.axis_index("z")
    core = lax.axis_index("core")
    down_blocks = jnp.roll(down_weight.reshape(ff_local, n_z, n_core, cols), (-zi, -core), (1, 2))
    down_perm = down_blocks.transpose(0, 2, 1, 3).reshape(ff_local, width)
    up_blocks = jnp.roll(up_weight.reshape(n_z, n_core, cols, ff_local), (-zi, -core), (0, 1))
    up_perm = up_blocks.transpose(1, 0, 2, 3).reshape(width, ff_local)
    share = width // n_core
    tok_half = lax.dynamic_slice_in_dim(tokens, core * share, share, 1)
    grad_half = lax.dynamic_slice_in_dim(grad_out, core * share, share, 1)
    grad_rows = (gate_values[:, :, None] * grad_half[:, None, :].astype(jnp.float32)).astype(
        jnp.bfloat16
    )
    grad_rows = grad_rows.reshape(pair_count, share)
    placed, _ = plan_slots(expert_ids, n_exp, capacity)
    summed = placed.reshape(n_exp * capacity, tok_count, top_k).sum(axis=2)
    rows_in, rows_grad = dispatch_rows((summed, placed), (tok_half, grad_rows), n_exp, capacity, n_core)
    out_part, dx_part, grad_up_e, grad_down_e = expert_math(
        rows_in, rows_grad, up_weight, down_weight, up_perm, down_perm
    )
    acc = reduce_over_rep(
        (out_part.astype(jnp.bfloat16), dx_part.astype(jnp.bfloat16)), n_z, n_core, cols
    )
    slots = n_exp * capacity
    back_both = lax.all_to_all(
        acc.astype(jnp.bfloat16).reshape(2, n_exp, capacity, cols),
        "exp",
        split_axis=1,
        concat_axis=1,
        tiled=True,
    )
    back_out = back_both[0].reshape(slots, cols)
    back_dx = back_both[1].reshape(slots, cols)
    pair_out = jnp.einsum(
        "st,sd->td",
        placed,
        back_out,
        preferred_element_type=jnp.float32,
    )
    pair_dx = jnp.einsum(
        "st,sd->td",
        placed,
        back_dx,
        preferred_element_type=jnp.float32,
    )
    mixed = jnp.sum(gate_values[:, :, None] * pair_out.reshape(tok_count, top_k, cols), axis=1)
    grad_tokens = jnp.sum(pair_dx.reshape(tok_count, top_k, cols), axis=1)
    return (
        mixed.astype(jnp.bfloat16),
        grad_tokens.astype(jnp.bfloat16),
        grad_up_e.astype(jnp.bfloat16)[None],
        grad_down_e.astype(jnp.bfloat16)[None],
    )


def solution(mesh):
    n_rep, n_exp = mesh.devices.shape
    n_core = 2
    mesh3 = Mesh(mesh.devices.reshape(n_rep // n_core, n_core, n_exp), ("z", "core", "exp"))
    rep = ("z", "core")
    return jax.shard_map(
        local,
        mesh=mesh3,
        in_specs=(
            P("exp", None),
            P("exp", None),
            P("exp", None),
            P("exp", None),
            P("exp", None, rep),
            P("exp", rep, None),
        ),
        out_specs=(P("exp", rep), P("exp", rep), P("exp", None, rep), P("exp", rep, None)),
        check_vma=False,
    )
```

```python
import jax
import jax.numpy as jnp
from jax import lax
from jax.sharding import Mesh, PartitionSpec as P


def plan_slots(routed, experts, capacity):
    flat_ids = routed.reshape(-1)
    onehot = (flat_ids[:, None] == jnp.arange(experts, dtype=jnp.int32)[None, :]).astype(jnp.int32)
    before = jnp.cumsum(onehot, axis=0) - onehot
    position = jnp.sum(before * onehot, axis=1)
    counts = jnp.sum(onehot, axis=0)
    slotting_labels = flat_ids * capacity + position
    placed = (
        slotting_labels[None, :] == jnp.arange(experts * capacity, dtype=jnp.int32)[:, None]
    ).astype(jnp.bfloat16)
    return (placed, counts)


def expert_math(rows_in, rows_grad, up_weight, down_weight, up_perm, down_perm):
    preact = jnp.dot(rows_in, up_weight, preferred_element_type=jnp.float32)
    sigmoid_val = jax.nn.sigmoid(preact)
    hidden_units = (preact * sigmoid_val).astype(jnp.bfloat16)
    out_part = jnp.dot(hidden_units, down_perm, preferred_element_type=jnp.float32)
    grad_hidden = lax.dot_general(
        rows_grad, down_weight, (((1,), (1,)), ((), ())), preferred_element_type=jnp.float32
    )
    slope = sigmoid_val * (1.0 + preact * (1.0 - sigmoid_val))
    gradient_before_activation = (grad_hidden * slope).astype(jnp.bfloat16)
    dx_part = lax.dot_general(
        gradient_before_activation,
        up_perm,
        (((1,), (1,)), ((), ())),
        preferred_element_type=jnp.float32,
    )
    grad_down_e = lax.dot_general(
        hidden_units, rows_grad, (((0,), (0,)), ((), ())), preferred_element_type=jnp.float32
    )
    grad_up_e = lax.dot_general(
        rows_in,
        gradient_before_activation,
        (((0,), (0,)), ((), ())),
        preferred_element_type=jnp.float32,
    )
    return (out_part, dx_part, grad_up_e, grad_down_e)


def pick(stacked, index, axis):
    return lax.dynamic_index_in_dim(stacked, index, axis=axis, keepdims=False)


def reduce_over_rep(parts, n_z, n_core, cols):
    share = n_z * cols
    swap = [(j, (j + 1) % n_core) for j in range(n_core)]
    pair_sum = jnp.concatenate(
        [
            (
                p[:, :share].astype(jnp.float32)
                + lax.ppermute(p[:, share:], "core", swap).astype(jnp.float32)
            ).astype(jnp.bfloat16)
            for p in parts
        ],
        axis=0,
    )
    block = [pair_sum[:, k * cols : (k + 1) * cols] for k in range(n_z)]
    acc = block[0].astype(jnp.float32)
    if n_z != 8:
        for k in range(1, n_z):
            moved = lax.ppermute(block[k], "z", [(j, (j + k) % n_z) for j in range(n_z)])
            acc = acc + moved.astype(jnp.float32)
        return acc

    def shift(x, k):
        return lax.ppermute(x, "z", [(j, (j + k) % n_z) for j in range(n_z)]).astype(jnp.float32)

    rows = pair_sum.shape[0]
    top = rows // 2
    near_up = shift(block[1], 1)
    near_down = shift(block[7], -1)
    via_up = shift(block[3], 1)
    via_down = shift(block[5], -1)
    far_up = shift(block[4][:top], 2)
    far_down = shift(block[4][top:], -2)
    zeros = jnp.zeros((rows - top, cols), jnp.float32)
    agg_up = block[2].astype(jnp.float32) + via_up + jnp.concatenate([far_up, zeros], axis=0)
    agg_down = block[6].astype(jnp.float32) + via_down + jnp.concatenate([zeros, far_down], axis=0)
    acc = acc + near_up + near_down
    acc = acc + shift(agg_up.astype(jnp.bfloat16), 2)
    acc = acc + shift(agg_down.astype(jnp.bfloat16), -2)
    return acc


def dispatch_rows(placements, sources, n_exp, capacity, n_core):
    core = lax.axis_index("core")
    share = sources[0].shape[1]
    sent = jnp.concatenate(
        [
            jnp.dot(placed_rows, source, preferred_element_type=jnp.float32).astype(jnp.bfloat16)
            for placed_rows, source in zip(placements, sources)
        ],
        axis=1,
    )
    got = lax.all_to_all(
        sent.reshape(n_exp, capacity, sent.shape[1]), "exp", split_axis=0, concat_axis=0, tiled=True
    ).reshape(n_exp * capacity, sent.shape[1])
    swap = [(j, (j + 1) % n_core) for j in range(n_core)]
    rows = []
    for i in range(len(sources)):
        mine = got[:, i * share : (i + 1) * share]
        other = lax.ppermute(mine, "core", swap)
        pair = jnp.stack([mine, other])
        rows.append(jnp.concatenate([pick(pair, core, 0), pick(pair, 1 - core, 0)], axis=1))
    return rows


def local(tokens, expert_ids, gate_values, grad_out, w_up, w_down):
    n_z = lax.axis_size("z")
    n_core = lax.axis_size("core")
    n_rep = n_z * n_core
    n_exp = lax.axis_size("exp")
    tok_count, width = tokens.shape
    top_k = expert_ids.shape[1]
    pair_count = tok_count * top_k
    capacity = max(2, min(tok_count, 2 * tok_count * top_k // n_exp))
    cols = width // n_rep
    up_weight = w_up[0]
    down_weight = w_down[0]
    ff_local = up_weight.shape[1]
    zi = lax.axis_index("z")
    core = lax.axis_index("core")
    down_blocks = jnp.roll(down_weight.reshape(ff_local, n_z, n_core, cols), (-zi, -core), (1, 2))
    down_perm = down_blocks.transpose(0, 2, 1, 3).reshape(ff_local, width)
    up_blocks = jnp.roll(up_weight.reshape(n_z, n_core, cols, ff_local), (-zi, -core), (0, 1))
    up_perm = up_blocks.transpose(1, 0, 2, 3).reshape(width, ff_local)
    share = width // n_core
    tok_half = lax.dynamic_slice_in_dim(tokens, core * share, share, 1)
    grad_half = lax.dynamic_slice_in_dim(grad_out, core * share, share, 1)
    grad_rows = (gate_values[:, :, None] * grad_half[:, None, :].astype(jnp.float32)).astype(
        jnp.bfloat16
    )
    grad_rows = grad_rows.reshape(pair_count, share)
    placed, _ = plan_slots(expert_ids, n_exp, capacity)
    summed = placed.reshape(n_exp * capacity, tok_count, top_k).sum(axis=2)
    rows_in, rows_grad = dispatch_rows((summed, placed), (tok_half, grad_rows), n_exp, capacity, n_core)
    out_part, dx_part, grad_up_e, grad_down_e = expert_math(
        rows_in, rows_grad, up_weight, down_weight, up_perm, down_perm
    )
    acc = reduce_over_rep(
        (out_part.astype(jnp.bfloat16), dx_part.astype(jnp.bfloat16)), n_z, n_core, cols
    )
    slots = n_exp * capacity
    back_both = lax.all_to_all(
        acc.astype(jnp.bfloat16).reshape(2, n_exp, capacity, cols),
        "exp",
        split_axis=1,
        concat_axis=1,
        tiled=True,
    )
    back_out = back_both[0].reshape(slots, cols)
    back_dx = back_both[1].reshape(slots, cols)
    pair_out = jnp.einsum(
        "st,sd->td",
        placed,
        back_out,
        preferred_element_type=jnp.float32,
    )
    pair_dx = jnp.einsum(
        "st,sd->td",
        placed,
        back_dx,
        preferred_element_type=jnp.float32,
    )
    mixed = jnp.sum(gate_values[:, :, None] * pair_out.reshape(tok_count, top_k, cols), axis=1)
    grad_tokens = jnp.sum(pair_dx.reshape(tok_count, top_k, cols), axis=1)
    return (
        mixed.astype(jnp.bfloat16),
        grad_tokens.astype(jnp.bfloat16),
        grad_up_e.astype(jnp.bfloat16)[None],
        grad_down_e.astype(jnp.bfloat16)[None],
    )


def solution(mesh):
    n_rep, n_exp = mesh.devices.shape
    n_core = 2
    mesh3 = Mesh(mesh.devices.reshape(n_rep // n_core, n_core, n_exp), ("z", "core", "exp"))
    rep = ("z", "core")
    return jax.shard_map(
        local,
        mesh=mesh3,
        in_specs=(
            P("exp", None),
            P("exp", None),
            P("exp", None),
            P("exp", None),
            P("exp", None, rep),
            P("exp", rep, None),
        ),
        out_specs=(P("exp", rep), P("exp", rep), P("exp", None, rep), P("exp", rep, None)),
        check_vma=False,
    )
```
